512 devices in a mesh: stretch: 32 (over y_hi, z), head: 8 (over x, y_lo), cfg: 2 (over core).
Axes of the slice: x: 4, y: 8 (y_hi: 4, y_lo: 2; y = y_hi * 2 + y_lo), z: 8, core: 2. Of those that a mesh axis runs over, the one named last changes fastest.
Arguments:
- queries: bfloat16 [57344, 5120], P(('cfg', 'stretch', 'head')), parts along dimension 0, may hold values from -6 to 6
- keys: bfloat16 [57344, 5120], P(('cfg', 'stretch', 'head')), parts along dimension 0, may hold values from -6 to 6
- values: bfloat16 [57344, 5120], P(('cfg', 'stretch', 'head')), parts along dimension 0, may hold values from -6 to 6
- frames: int32 [32], replicated, may hold values from 4 to 7, as said below
- motion: int32 [32], replicated, may hold values from 0 to 4, as said below
Outputs:
- attended: bfloat16 [57344, 5120], P(('cfg', 'stretch', 'head')), parts along dimension 0
The draws below stay inside these ranges and needn't reach their ends.
There are 2 independent parts, one for each index of `cfg`. The reference program is written for one: setup_inputs(seed, part) draws one part's arguments, and reference() takes and returns one part's arrays. A program takes and returns all parts, laid end to end along the dimension named above; an argument that names none is the same for every part. Nothing has to cross between parts.
Inputs may be any that keep to these rules, and one draw needn't show every extreme that they name: Every stretch holds at least 4 frames; some stretch holds 7. `motion`: stretch 0 takes none; some stretch takes 4.
All inputs are finite; a program needn't handle non-finite values.
Results may differ from the reference program's by a relative error of at most 0.0046.
Values may be sent and summed in bfloat16 or wider, within the bound.
No kernel may reach another device: no remote copies, remote signals or barrier semaphores. Data moves between devices by JAX's collectives and lax.ppermute only.
A program may use at most 128 MiB of HBM per device.

```python
import math
import jax
import jax.numpy as jnp
from jax import lax

HEADS = 40
HD = 128
FT = 128
FRAMES = 7
MOT_CAP = 4
STRETCHES = 32
TOKENS = 28672


def base_field(key, salt):
    inner = jax.random.fold_in(key, salt)
    raw = jax.random.normal(jax.random.fold_in(inner, 1), (TOKENS, HEADS * HD), jnp.float32)
    return raw


def draw_queries(key, part):
    field = base_field(key, 3)
    return jnp.clip(field, -6.0, 6.0).astype(jnp.bfloat16)


def draw_keys(key, part):
    field = base_field(key, 4)
    return jnp.clip(field, -6.0, 6.0).astype(jnp.bfloat16)


def draw_values(key, part):
    field = base_field(key, 5)
    return jnp.clip(field, -6.0, 6.0).astype(jnp.bfloat16)


def draw_frames(key, part):
    counts = jax.random.randint(jax.random.fold_in(key, 5), (STRETCHES,), MOT_CAP, FRAMES + 1)
    fullest = jax.random.randint(jax.random.fold_in(key, 6), (), 0, STRETCHES)
    return counts.at[fullest].set(FRAMES).astype(jnp.int32)


def draw_motion(key, part):
    counts = jax.random.randint(jax.random.fold_in(key, 8), (STRETCHES,), 1, MOT_CAP + 1)
    most = jax.random.randint(jax.random.fold_in(key, 9), (), 1, STRETCHES)
    counts = counts.at[most].set(MOT_CAP)
    return counts.at[0].set(0).astype(jnp.int32)


def setup_inputs(seed: int = 0, part: int = 0) -> dict:
    splits = jax.random.split(jax.random.key(seed), 6)
    part_splits = jax.random.split(jax.random.fold_in(splits[5], part), 6)
    queries = draw_queries(jax.random.fold_in(jax.random.fold_in(splits[5], part), 71), part)
    keys = draw_keys(jax.random.fold_in(jax.random.fold_in(splits[5], part), 71), part)
    values = draw_values(jax.random.fold_in(jax.random.fold_in(splits[5], part), 71), part)
    frames = draw_frames(jax.random.fold_in(splits[5], 71), part)
    motion = draw_motion(jax.random.fold_in(splits[5], 71), part)
    return {"queries": queries, "keys": keys, "values": values, "frames": frames, "motion": motion}


NEG = -1e+30

def head_block(q_head, k_head, v_head, key_live):
    scores = lax.dot_general(q_head, k_head, (((1,), (1,)), ((), ())), preferred_element_type=jnp.float32)
    scores = scores * (1.0 / math.sqrt(q_head.shape[1]))
    masked = jnp.where(key_live[None, :], scores, NEG)
    top = lax.optimization_barrier(jnp.max(masked, axis=1))
    weights = jnp.where(key_live[None, :], jnp.exp(masked - top[:, None]), 0.0)
    total = lax.optimization_barrier(jnp.sum(weights, axis=1))
    acc = jnp.dot(weights.astype(jnp.bfloat16), v_head, preferred_element_type=jnp.float32)
    return (top, total, acc)

def pick_head(array, index):
    return lax.dynamic_index_in_dim(array, index, 1, keepdims=False)

def own_part(queries, keys, values, key_live):
    rows, count, width = queries.shape
    start = (jnp.zeros((rows, count), jnp.float32), jnp.zeros((rows, count), jnp.float32), jnp.zeros((rows, count, width), jnp.float32))

    def step(index, carry):
        tops, totals, accs = carry
        top, total, acc = head_block(pick_head(queries, index), pick_head(keys, index), pick_head(values, index), key_live)
        tops = lax.dynamic_update_index_in_dim(tops, top, index, 1)
        totals = lax.dynamic_update_index_in_dim(totals, total, index, 1)
        accs = lax.dynamic_update_index_in_dim(accs, acc, index, 1)
        return (tops, totals, accs)
    return lax.fori_loop(0, count, step, start)

def finish(queries, motion_keys, motion_values, motion_live, query_live, partial_value):
    tops, totals, accs = partial_value
    count = queries.shape[1]

    def step(index, result):
        top, total, acc = head_block(pick_head(queries, index), pick_head(motion_keys, index), pick_head(motion_values, index), motion_live)
        top_own = pick_head(tops, index)
        total_own = pick_head(totals, index)
        acc_own = pick_head(accs, index)
        peak = jnp.maximum(top_own, top)
        factor_own = jnp.exp(top_own - peak)
        factor_mot = jnp.exp(top - peak)
        mixed = (acc_own * factor_own[:, None] + acc * factor_mot[:, None]) / (total_own * factor_own + total * factor_mot)[:, None]
        mixed = jnp.where(query_live[:, None], mixed, 0.0).astype(jnp.bfloat16)
        return lax.dynamic_update_index_in_dim(result, mixed, index, 1)
    return lax.fori_loop(0, count, step, jnp.zeros(queries.shape, jnp.bfloat16))

def reference(queries, keys, values, frames, motion):
    width = queries.shape[1]
    span = FRAMES * FT
    tail = MOT_CAP * FT
    spot = jnp.arange(span, dtype=jnp.int32) // FT
    slot = jnp.arange(tail, dtype=jnp.int32) // FT

    def take(array, begin, length):
        return lax.dynamic_slice_in_dim(array, begin, length, 0).reshape(length, HEADS, HD)

    def one_stretch(index):
        begin = (index * span).astype(jnp.int32)
        prior = jnp.maximum(index - 1, 0).astype(jnp.int32)
        tail_begin = (prior * span + (frames[prior] - MOT_CAP) * FT).astype(jnp.int32)
        live = spot < frames[index]
        motion_live = slot >= MOT_CAP - motion[index]
        q_stretch = take(queries, begin, span)
        partial_value = own_part(q_stretch, take(keys, begin, span), take(values, begin, span), live)
        mixed = finish(q_stretch, take(keys, tail_begin, tail), take(values, tail_begin, tail), motion_live, live, partial_value)
        return mixed.reshape(span, width)
    blocks = lax.map(one_stretch, jnp.arange(STRETCHES, dtype=jnp.int32))
    return blocks.reshape(STRETCHES * span, width)
```

```python
import functools
import math

import jax
import jax.numpy as jnp
from jax import lax
from jax.experimental import pallas as pl
from jax.experimental.pallas import tpu as pltpu
from jax.sharding import PartitionSpec as P

HD = 128
FT = 128
MOT_CAP = 4

NEG = -1e30
TQ = 448


def from_behind(shard, axis, by):
    size = lax.axis_size(axis)
    pairs = [(i, i + by) for i in range(size) if 0 <= i + by < size]
    return lax.ppermute(shard, axis, pairs)


def softmax_part(q, k, v, live):
    scores = lax.dot_general(
        q, k, (((1,), (1,)), ((), ())), preferred_element_type=jnp.float32
    )
    scores = scores * (1.0 / math.sqrt(HD))
    masked = jnp.where(live, scores, NEG)
    top = jnp.max(masked, axis=1, keepdims=True)
    weights = jnp.where(live, jnp.exp(masked - top), 0.0)
    total = jnp.sum(weights, axis=1, keepdims=True)
    acc = jnp.dot(weights.astype(jnp.bfloat16), v, preferred_element_type=jnp.float32)
    return top, total, acc


def attend_kernel(counts, q_ref, k_ref, v_ref, mk_ref, mv_ref, o_ref):
    own_live = counts[0] * FT
    mot_start = (MOT_CAP - counts[1]) * FT
    row0 = pl.program_id(1) * TQ
    q = q_ref[...]
    span = k_ref.shape[0]
    tail = mk_ref.shape[0]
    key_live = lax.broadcasted_iota(jnp.int32, (1, span), 1) < own_live
    slot_live = lax.broadcasted_iota(jnp.int32, (1, tail), 1) >= mot_start
    top_own, total_own, acc_own = softmax_part(q, k_ref[...], v_ref[...], key_live)
    top_mot, total_mot, acc_mot = softmax_part(q, mk_ref[...], mv_ref[...], slot_live)
    peak = jnp.maximum(top_own, top_mot)
    factor_own = jnp.exp(top_own - peak)
    factor_mot = jnp.exp(top_mot - peak)
    mixed = (acc_own * factor_own + acc_mot * factor_mot) / (
        total_own * factor_own + total_mot * factor_mot
    )
    rows = row0 + lax.broadcasted_iota(jnp.int32, (TQ, 1), 0)
    o_ref[...] = jnp.where(rows < own_live, mixed, 0.0).astype(o_ref.dtype)


def attend(counts, q, k, v, mk, mv):
    span, local = q.shape
    tail = mk.shape[0]
    heads = local // HD
    grid = (heads, span // TQ)
    flops = heads * 4 * span * (span + tail) * HD
    cost = pl.CostEstimate(
        flops=flops,
        transcendentals=heads * span * (span + tail),
        bytes_accessed=(4 * span + 2 * tail) * local * 2,
    )
    return pl.pallas_call(
        attend_kernel,
        out_shape=jax.ShapeDtypeStruct((span, local), jnp.bfloat16),
        grid_spec=pltpu.PrefetchScalarGridSpec(
            num_scalar_prefetch=1,
            grid=grid,
            in_specs=[
                pl.BlockSpec((TQ, HD), lambda h, i, c: (i, h)),
                pl.BlockSpec((span, HD), lambda h, i, c: (0, h)),
                pl.BlockSpec((span, HD), lambda h, i, c: (0, h)),
                pl.BlockSpec((tail, HD), lambda h, i, c: (0, h)),
                pl.BlockSpec((tail, HD), lambda h, i, c: (0, h)),
            ],
            out_specs=pl.BlockSpec((TQ, HD), lambda h, i, c: (i, h)),
        ),
        compiler_params=pltpu.CompilerParams(
            dimension_semantics=("arbitrary", "arbitrary"),
        ),
        cost_estimate=cost,
    )(counts, q, k, v, mk, mv)


def body(queries, keys, values, frames, motion):
    stretch_index = lax.axis_index("stretch")
    tail = MOT_CAP * FT
    count_own = frames[stretch_index]
    counts = jnp.stack([count_own, motion[stretch_index]]).astype(jnp.int32)
    tail_begin = (count_own - MOT_CAP) * FT
    k_heads = lax.all_to_all(keys, "head", split_axis=1, concat_axis=0, tiled=True)
    v_heads = lax.all_to_all(values, "head", split_axis=1, concat_axis=0, tiled=True)
    k_tail = lax.dynamic_slice_in_dim(k_heads, tail_begin, tail, 0)
    v_tail = lax.dynamic_slice_in_dim(v_heads, tail_begin, tail, 0)
    k_prior, v_prior = from_behind((k_tail, v_tail), "stretch", 1)
    q_heads = lax.all_to_all(queries, "head", split_axis=1, concat_axis=0, tiled=True)
    mixed = attend(counts, q_heads, k_heads, v_heads, k_prior, v_prior)
    return lax.all_to_all(mixed, "head", split_axis=0, concat_axis=1, tiled=True)


def solution(mesh):
    placed = (
        P(("cfg", "stretch", "head"), None),
        P(("cfg", "stretch", "head"), None),
        P(("cfg", "stretch", "head"), None),
        P(),
        P(),
    )
    return jax.shard_map(
        body,
        mesh=mesh,
        in_specs=placed,
        out_specs=P(("cfg", "stretch", "head"), None),
        check_vma=False,
    )
```

```python
import math

import jax
import jax.numpy as jnp
from jax import lax
from jax.experimental import pallas as pl
from jax.experimental.pallas import tpu as pltpu
from jax.sharding import PartitionSpec as P

HD = 128
FT = 128
MOT_CAP = 4

NEG = -1e30
TQ = 448


def from_behind(shard, axis, by):
    size = lax.axis_size(axis)
    pairs = [(i, i + by) for i in range(size) if 0 <= i + by < size]
    return lax.ppermute(shard, axis, pairs)


def softmax_part(q, k, v, live):
    scores = lax.dot_general(
        q, k, (((1,), (1,)), ((), ())), preferred_element_type=jnp.float32
    )
    scores = scores * (1.0 / math.sqrt(HD))
    masked = jnp.where(live, scores, NEG)
    top = jnp.max(masked, axis=1, keepdims=True)
    weights = jnp.exp(masked - top)
    total = jnp.sum(weights, axis=1, keepdims=True)
    acc = jnp.dot(weights.astype(jnp.bfloat16), v, preferred_element_type=jnp.float32)
    return top, total, acc


def own_kernel(counts, q_ref, k_ref, v_ref, acc_ref, top_ref, tot_ref):
    own_live = counts[0] * FT
    span = k_ref.shape[0]
    key_live = lax.broadcasted_iota(jnp.int32, (1, span), 1) < own_live
    top, total, acc = softmax_part(q_ref[...], k_ref[...], v_ref[...], key_live)
    acc_ref[...] = acc
    top_ref[...] = jnp.broadcast_to(top, top_ref.shape)
    tot_ref[...] = jnp.broadcast_to(total, tot_ref.shape)


def finish_kernel(counts, q_ref, mk_ref, mv_ref, acc_ref, top_ref, tot_ref, o_ref):
    own_live = counts[0] * FT
    mot_start = (MOT_CAP - counts[1]) * FT
    tail = mk_ref.shape[0]
    slot_live = lax.broadcasted_iota(jnp.int32, (1, tail), 1) >= mot_start
    top_mot, total_mot, acc_mot = softmax_part(
        q_ref[...], mk_ref[...], mv_ref[...], slot_live
    )
    top_own = top_ref[:, 0:1]
    total_own = tot_ref[:, 0:1]
    peak = jnp.maximum(top_own, top_mot)
    factor_own = jnp.exp(top_own - peak)
    factor_mot = jnp.exp(top_mot - peak)
    mixed = (acc_ref[...] * factor_own + acc_mot * factor_mot) / (
        total_own * factor_own + total_mot * factor_mot
    )
    rows = pl.program_id(1) * TQ + lax.broadcasted_iota(jnp.int32, (TQ, 1), 0)
    o_ref[...] = jnp.where(rows < own_live, mixed, 0.0).astype(o_ref.dtype)


def row_block(h, i, c):
    return (i, h)


def own_part(counts, q, kv):
    span, local = q.shape
    heads = local // HD
    part = jax.ShapeDtypeStruct((span, local), jnp.float32)
    cost = pl.CostEstimate(
        flops=heads * 4 * span * span * HD,
        transcendentals=heads * span * span,
        bytes_accessed=3 * span * local * 2 + 3 * span * local * 4,
    )
    return pl.pallas_call(
        own_kernel,
        out_shape=(part, part, part),
        grid_spec=pltpu.PrefetchScalarGridSpec(
            num_scalar_prefetch=1,
            grid=(heads, span // TQ),
            in_specs=[
                pl.BlockSpec((TQ, HD), row_block),
                pl.BlockSpec((None, span, HD), lambda h, i, c: (0, 0, h)),
                pl.BlockSpec((None, span, HD), lambda h, i, c: (1, 0, h)),
            ],
            out_specs=[pl.BlockSpec((TQ, HD), row_block)] * 3,
        ),
        compiler_params=pltpu.CompilerParams(
            dimension_semantics=("arbitrary", "arbitrary"),
        ),
        cost_estimate=cost,
    )(counts, q, kv, kv)


def finish_part(counts, q, kv_tail, acc, top, tot):
    span, local = q.shape
    tail = kv_tail.shape[1]
    heads = local // HD
    cost = pl.CostEstimate(
        flops=heads * 4 * span * tail * HD,
        transcendentals=heads * span * tail,
        bytes_accessed=2 * span * local * 2 + 2 * tail * local * 2 + 3 * span * local * 4,
    )
    return pl.pallas_call(
        finish_kernel,
        out_shape=jax.ShapeDtypeStruct((span, local), jnp.bfloat16),
        grid_spec=pltpu.PrefetchScalarGridSpec(
            num_scalar_prefetch=1,
            grid=(heads, span // TQ),
            in_specs=[
                pl.BlockSpec((TQ, HD), row_block),
                pl.BlockSpec((None, tail, HD), lambda h, i, c: (0, 0, h)),
                pl.BlockSpec((None, tail, HD), lambda h, i, c: (1, 0, h)),
                pl.BlockSpec((TQ, HD), row_block),
                pl.BlockSpec((TQ, HD), row_block),
                pl.BlockSpec((TQ, HD), row_block),
            ],
            out_specs=pl.BlockSpec((TQ, HD), row_block),
        ),
        compiler_params=pltpu.CompilerParams(
            dimension_semantics=("arbitrary", "arbitrary"),
        ),
        cost_estimate=cost,
    )(counts, q, kv_tail, kv_tail, acc, top, tot)


def body(queries, keys, values, frames, motion):
    stretch_index = lax.axis_index("stretch")
    tail = MOT_CAP * FT
    count_own = frames[stretch_index]
    counts = jnp.stack([count_own, motion[stretch_index]]).astype(jnp.int32)
    tail_begin = (count_own - MOT_CAP) * FT
    kv = jnp.stack([keys, values])
    kv_heads = lax.all_to_all(kv, "head", split_axis=2, concat_axis=1, tiled=True)
    kv_tail = lax.dynamic_slice_in_dim(kv_heads, tail_begin, tail, 1)
    kv_prior = from_behind(kv_tail, "stretch", 1)
    q_heads = lax.all_to_all(queries, "head", split_axis=1, concat_axis=0, tiled=True)
    acc, top, tot = own_part(counts, q_heads, kv_heads)
    mixed = finish_part(counts, q_heads, kv_prior, acc, top, tot)
    return lax.all_to_all(mixed, "head", split_axis=0, concat_axis=1, tiled=True)


def solution(mesh):
    placed = (
        P(("cfg", "stretch", "head"), None),
        P(("cfg", "stretch", "head"), None),
        P(("cfg", "stretch", "head"), None),
        P(),
        P(),
    )
    return jax.shard_map(
        body,
        mesh=mesh,
        in_specs=placed,
        out_specs=P(("cfg", "stretch", "head"), None),
        check_vma=False,
    )
```

```python
import math

import jax
import jax.numpy as jnp
from jax import lax
from jax.experimental import pallas as pl
from jax.experimental.pallas import tpu as pltpu
from jax.sharding import PartitionSpec as P

HD = 128
FT = 128
MOT_CAP = 4

NEG = -1e30
TQ = 448


def from_behind(shard, axis, by):
    size = lax.axis_size(axis)
    pairs = [(i, i + by) for i in range(size) if 0 <= i + by < size]
    return lax.ppermute(shard, axis, pairs)


def softmax_part(q, k, v, live):
    scores = lax.dot_general(
        q, k, (((1,), (1,)), ((), ())), preferred_element_type=jnp.float32
    )
    scores = scores * (1.0 / math.sqrt(HD))
    masked = jnp.where(live, scores, NEG)
    top = jnp.max(masked, axis=1, keepdims=True)
    weights = jnp.exp(masked - top).astype(jnp.bfloat16)
    v_ext = jnp.concatenate([v, jnp.ones_like(v)], axis=1)
    both = jnp.dot(weights, v_ext, preferred_element_type=jnp.float32)
    return top, both[:, HD : HD + 1], both[:, :HD]


def own_kernel(counts, q_ref, k_ref, v_ref, acc_ref, top_ref, tot_ref):
    own_live = counts[0] * FT
    span = k_ref.shape[0]
    key_live = lax.broadcasted_iota(jnp.int32, (1, span), 1) < own_live
    top, total, acc = softmax_part(q_ref[...], k_ref[...], v_ref[...], key_live)
    acc_ref[...] = acc
    top_ref[...] = jnp.broadcast_to(top, top_ref.shape)
    tot_ref[...] = jnp.broadcast_to(total, tot_ref.shape)


def finish_kernel(counts, q_ref, mk_ref, mv_ref, acc_ref, top_ref, tot_ref, o_ref):
    own_live = counts[0] * FT
    mot_start = (MOT_CAP - counts[1]) * FT
    tail = mk_ref.shape[0]
    slot_live = lax.broadcasted_iota(jnp.int32, (1, tail), 1) >= mot_start
    top_mot, total_mot, acc_mot = softmax_part(
        q_ref[...], mk_ref[...], mv_ref[...], slot_live
    )
    top_own = top_ref[:, 0:1]
    total_own = tot_ref[:, 0:1]
    peak = jnp.maximum(top_own, top_mot)
    factor_own = jnp.exp(top_own - peak)
    factor_mot = jnp.exp(top_mot - peak)
    mixed = (acc_ref[...] * factor_own + acc_mot * factor_mot) / (
        total_own * factor_own + total_mot * factor_mot
    )
    rows = pl.program_id(1) * TQ + lax.broadcasted_iota(jnp.int32, (TQ, 1), 0)
    o_ref[...] = jnp.where(rows < own_live, mixed, 0.0).astype(o_ref.dtype)


def row_block(h, i, c):
    return (i, h)


def own_part(counts, q, k, v):
    span, local = q.shape
    heads = local // HD
    part = jax.ShapeDtypeStruct((span, local), jnp.float32)
    cost = pl.CostEstimate(
        flops=heads * 4 * span * span * HD,
        transcendentals=heads * span * span,
        bytes_accessed=3 * span * local * 2 + 3 * span * local * 4,
    )
    return pl.pallas_call(
        own_kernel,
        out_shape=(part, part, part),
        grid_spec=pltpu.PrefetchScalarGridSpec(
            num_scalar_prefetch=1,
            grid=(heads, span // TQ),
            in_specs=[
                pl.BlockSpec((TQ, HD), row_block),
                pl.BlockSpec((span, HD), lambda h, i, c: (0, h)),
                pl.BlockSpec((span, HD), lambda h, i, c: (0, h)),
            ],
            out_specs=[pl.BlockSpec((TQ, HD), row_block)] * 3,
        ),
        compiler_params=pltpu.CompilerParams(
            dimension_semantics=("arbitrary", "arbitrary"),
        ),
        cost_estimate=cost,
    )(counts, q, k, v)


def finish_part(counts, q, mk, mv, acc, top, tot):
    span, local = q.shape
    tail = mk.shape[0]
    heads = local // HD
    cost = pl.CostEstimate(
        flops=heads * 4 * span * tail * HD,
        transcendentals=heads * span * tail,
        bytes_accessed=2 * span * local * 2 + 2 * tail * local * 2 + 3 * span * local * 4,
    )
    return pl.pallas_call(
        finish_kernel,
        out_shape=jax.ShapeDtypeStruct((span, local), jnp.bfloat16),
        grid_spec=pltpu.PrefetchScalarGridSpec(
            num_scalar_prefetch=1,
            grid=(heads, span // TQ),
            in_specs=[
                pl.BlockSpec((TQ, HD), row_block),
                pl.BlockSpec((tail, HD), lambda h, i, c: (0, h)),
                pl.BlockSpec((tail, HD), lambda h, i, c: (0, h)),
                pl.BlockSpec((TQ, HD), row_block),
                pl.BlockSpec((TQ, HD), row_block),
                pl.BlockSpec((TQ, HD), row_block),
            ],
            out_specs=pl.BlockSpec((TQ, HD), row_block),
        ),
        compiler_params=pltpu.CompilerParams(
            dimension_semantics=("arbitrary", "arbitrary"),
        ),
        cost_estimate=cost,
    )(counts, q, mk, mv, acc, top, tot)


def body(queries, keys, values, frames, motion):
    stretch_index = lax.axis_index("stretch")
    tail = MOT_CAP * FT
    count_own = frames[stretch_index]
    counts = jnp.stack([count_own, motion[stretch_index]]).astype(jnp.int32)
    tail_begin = (count_own - MOT_CAP) * FT
    k_heads = lax.all_to_all(keys, "head", split_axis=1, concat_axis=0, tiled=True)
    k_tail = lax.dynamic_slice_in_dim(k_heads, tail_begin, tail, 0)
    k_prior = from_behind(k_tail, "stretch", 1)
    v_heads = lax.all_to_all(values, "head", split_axis=1, concat_axis=0, tiled=True)
    v_tail = lax.dynamic_slice_in_dim(v_heads, tail_begin, tail, 0)
    v_prior = from_behind(v_tail, "stretch", 1)
    q_heads = lax.all_to_all(queries, "head", split_axis=1, concat_axis=0, tiled=True)
    acc, top, tot = own_part(counts, q_heads, k_heads, v_heads)
    mixed = finish_part(counts, q_heads, k_prior, v_prior, acc, top, tot)
    return lax.all_to_all(mixed, "head", split_axis=0, concat_axis=1, tiled=True)


def solution(mesh):
    placed = (
        P(("cfg", "stretch", "head"), None),
        P(("cfg", "stretch", "head"), None),
        P(("cfg", "stretch", "head"), None),
        P(),
        P(),
    )
    return jax.shard_map(
        body,
        mesh=mesh,
        in_specs=placed,
        out_specs=P(("cfg", "stretch", "head"), None),
        check_vma=False,
    )
```

```python
import math

import jax
import jax.numpy as jnp
from jax import lax
from jax.experimental import pallas as pl
from jax.experimental.pallas import tpu as pltpu
from jax.sharding import PartitionSpec as P

HD = 128
FT = 128
MOT_CAP = 4

NEG = -1e30
TQ = 448
COLS = 8


def from_behind(shard, axis, by):
    size = lax.axis_size(axis)
    pairs = [(i, i + by) for i in range(size) if 0 <= i + by < size]
    return lax.ppermute(shard, axis, pairs)


def scaled_scores(q, k, live):
    scores = lax.dot_general(
        q, k, (((1,), (1,)), ((), ())), preferred_element_type=jnp.float32
    )
    scores = scores * (1.0 / math.sqrt(HD))
    return jnp.where(live, scores, NEG)


def head_cols(h):
    return slice(h * HD, (h + 1) * HD)


def own_kernel(counts, q_ref, k_ref, v_ref, acc_ref, top_ref, tot_ref):
    own_live = counts[0] * FT
    span = k_ref.shape[0]
    key_live = lax.broadcasted_iota(jnp.int32, (1, span), 1) < own_live
    for h in range(acc_ref.shape[1] // HD):
        c = head_cols(h)
        masked = scaled_scores(q_ref[:, c], k_ref[:, c], key_live)
        top = jnp.max(masked, axis=1, keepdims=True)
        weights = jnp.exp(masked - top).astype(jnp.bfloat16)
        v = v_ref[:, c]
        v_ext = jnp.concatenate([v, jnp.ones_like(v)], axis=1)
        both = jnp.dot(weights, v_ext, preferred_element_type=jnp.float32)
        acc_ref[:, c] = both[:, :HD]
        top_ref[:, h : h + 1] = top
        tot_ref[:, h : h + 1] = both[:, HD : HD + 1]


def mscore_kernel(counts, q_ref, mk_ref, w_ref, top_ref, tot_ref):
    mot_start = (MOT_CAP - counts[1]) * FT
    tail = mk_ref.shape[0]
    slot_live = lax.broadcasted_iota(jnp.int32, (1, tail), 1) >= mot_start
    ones = jnp.ones((tail, HD), jnp.bfloat16)
    for h in range(q_ref.shape[1] // HD):
        c = head_cols(h)
        masked = scaled_scores(q_ref[:, c], mk_ref[:, c], slot_live)
        top = jnp.max(masked, axis=1, keepdims=True)
        weights = jnp.exp(masked - top).astype(jnp.bfloat16)
        w_ref[:, h * tail : (h + 1) * tail] = weights
        total = jnp.dot(weights, ones, preferred_element_type=jnp.float32)
        top_ref[:, h : h + 1] = top
        tot_ref[:, h : h + 1] = total[:, 0:1]


def merge_kernel(
    counts, w_ref, mv_ref, acc_ref, top_ref, tot_ref, mtop_ref, mtot_ref, o_ref
):
    own_live = counts[0] * FT
    tail = mv_ref.shape[0]
    rows = pl.program_id(0) * TQ + lax.broadcasted_iota(jnp.int32, (TQ, 1), 0)
    row_live = rows < own_live
    for h in range(o_ref.shape[1] // HD):
        c = head_cols(h)
        acc_mot = jnp.dot(
            w_ref[:, h * tail : (h + 1) * tail],
            mv_ref[:, c],
            preferred_element_type=jnp.float32,
        )
        top_own = top_ref[:, h : h + 1]
        top_mot = mtop_ref[:, h : h + 1]
        peak = jnp.maximum(top_own, top_mot)
        factor_own = jnp.exp(top_own - peak)
        factor_mot = jnp.exp(top_mot - peak)
        mixed = (acc_ref[:, c] * factor_own + acc_mot * factor_mot) / (
            tot_ref[:, h : h + 1] * factor_own + mtot_ref[:, h : h + 1] * factor_mot
        )
        o_ref[:, c] = jnp.where(row_live, mixed, 0.0).astype(o_ref.dtype)


def rows_of(width):
    return pl.BlockSpec((TQ, width), lambda i, c: (i, 0))


def whole(rows, width):
    return pl.BlockSpec((rows, width), lambda i, c: (0, 0))


def call(kernel, counts, operands, in_specs, outs, cost):
    span = operands[0].shape[0]
    shapes = [jax.ShapeDtypeStruct((span, w), t) for w, t in outs]
    return pl.pallas_call(
        kernel,
        out_shape=tuple(shapes),
        grid_spec=pltpu.PrefetchScalarGridSpec(
            num_scalar_prefetch=1,
            grid=(span // TQ,),
            in_specs=in_specs,
            out_specs=[rows_of(w) for w, _ in outs],
        ),
        compiler_params=pltpu.CompilerParams(dimension_semantics=("arbitrary",)),
        cost_estimate=cost,
    )(counts, *operands)


def body(queries, keys, values, frames, motion):
    stretch_index = lax.axis_index("stretch")
    tail = MOT_CAP * FT
    count_own = frames[stretch_index]
    counts = jnp.stack([count_own, motion[stretch_index]]).astype(jnp.int32)
    tail_begin = (count_own - MOT_CAP) * FT
    k_heads = lax.all_to_all(keys, "head", split_axis=1, concat_axis=0, tiled=True)
    v_heads = lax.all_to_all(values, "head", split_axis=1, concat_axis=0, tiled=True)
    k_tail = lax.dynamic_slice_in_dim(k_heads, tail_begin, tail, 0)
    v_tail = lax.dynamic_slice_in_dim(v_heads, tail_begin, tail, 0)
    k_prior = from_behind(k_tail, "stretch", 1)
    v_prior = from_behind(v_tail, "stretch", 1)
    q_heads = lax.all_to_all(queries, "head", split_axis=1, concat_axis=0, tiled=True)
    span, local = q_heads.shape
    heads = local // HD
    f32 = jnp.float32
    acc, top, tot = call(
        own_kernel,
        counts,
        (q_heads, k_heads, v_heads),
        [rows_of(local), whole(span, local), whole(span, local)],
        [(local, f32), (COLS, f32), (COLS, f32)],
        pl.CostEstimate(
            flops=heads * 2 * span * span * 3 * HD,
            transcendentals=heads * span * span,
            bytes_accessed=3 * span * local * 2 + span * local * 4,
        ),
    )
    w_mot, mtop, mtot = call(
        mscore_kernel,
        counts,
        (q_heads, k_prior),
        [rows_of(local), whole(tail, local)],
        [(heads * tail, jnp.bfloat16), (COLS, f32), (COLS, f32)],
        pl.CostEstimate(
            flops=heads * 2 * span * tail * 2 * HD,
            transcendentals=heads * span * tail,
            bytes_accessed=span * local * 2 + tail * local * 2 + span * heads * tail * 2,
        ),
    )
    (mixed,) = call(
        merge_kernel,
        counts,
        (w_mot, v_prior, acc, top, tot, mtop, mtot),
        [
            rows_of(heads * tail),
            whole(tail, local),
            rows_of(local),
            rows_of(COLS),
            rows_of(COLS),
            rows_of(COLS),
            rows_of(COLS),
        ],
        [(local, jnp.bfloat16)],
        pl.CostEstimate(
            flops=heads * 2 * span * tail * HD,
            transcendentals=2 * heads * span,
            bytes_accessed=span * heads * tail * 2 + span * local * 6 + tail * local * 2,
        ),
    )
    return lax.all_to_all(mixed, "head", split_axis=0, concat_axis=1, tiled=True)


def solution(mesh):
    placed = (
        P(("cfg", "stretch", "head"), None),
        P(("cfg", "stretch", "head"), None),
        P(("cfg", "stretch", "head"), None),
        P(),
        P(),
    )
    return jax.shard_map(
        body,
        mesh=mesh,
        in_specs=placed,
        out_specs=P(("cfg", "stretch", "head"), None),
        check_vma=False,
    )
```

```python
import functools
import math

import jax
import jax.numpy as jnp
from jax import lax
from jax.experimental import pallas as pl
from jax.experimental.pallas import tpu as pltpu
from jax.sharding import PartitionSpec as P

HD = 128
FT = 128
MOT_CAP = 4

NEG = -1e30
TQ = 448
COLS = 8


def from_behind(shard, axis, by):
    size = lax.axis_size(axis)
    pairs = [(i, i + by) for i in range(size) if 0 <= i + by < size]
    return lax.ppermute(shard, axis, pairs)


def scaled_scores(q, k, live):
    scores = lax.dot_general(
        q, k, (((1,), (1,)), ((), ())), preferred_element_type=jnp.float32
    )
    scores = scores * (1.0 / math.sqrt(HD))
    return jnp.where(live, scores, NEG)


def head_cols(h):
    return slice(h * HD, (h + 1) * HD)


def own_kernel(counts, q_ref, k_ref, v_ref, acc_ref, top_ref, tot_ref):
    own_live = counts[0] * FT
    span = k_ref.shape[0]
    key_live = lax.broadcasted_iota(jnp.int32, (1, span), 1) < own_live
    for h in range(acc_ref.shape[1] // HD):
        c = head_cols(h)
        masked = scaled_scores(q_ref[:, c], k_ref[:, c], key_live)
        top = jnp.max(masked, axis=1, keepdims=True)
        weights = jnp.exp(masked - top).astype(jnp.bfloat16)
        v = v_ref[:, c]
        v_ext = jnp.concatenate([v, jnp.ones_like(v)], axis=1)
        both = jnp.dot(weights, v_ext, preferred_element_type=jnp.float32)
        acc_ref[:, c] = both[:, :HD]
        top_ref[:, h : h + 1] = top
        tot_ref[:, h : h + 1] = both[:, HD : HD + 1]


def mscore_kernel(counts, q_ref, mk_ref, w_ref, top_ref, tot_ref):
    mot_start = (MOT_CAP - counts[1]) * FT
    tail = mk_ref.shape[0]
    slot_live = lax.broadcasted_iota(jnp.int32, (1, tail), 1) >= mot_start
    ones = jnp.ones((tail, HD), jnp.bfloat16)
    for h in range(q_ref.shape[1] // HD):
        c = head_cols(h)
        masked = scaled_scores(q_ref[:, c], mk_ref[:, c], slot_live)
        top = jnp.max(masked, axis=1, keepdims=True)
        weights = jnp.exp(masked - top).astype(jnp.bfloat16)
        w_ref[:, h * tail : (h + 1) * tail] = weights
        total = jnp.dot(weights, ones, preferred_element_type=jnp.float32)
        top_ref[:, h : h + 1] = top
        tot_ref[:, h : h + 1] = total[:, 0:1]


def merge_kernel(
    counts, w_ref, mv_ref, acc_ref, top_ref, tot_ref, mtop_ref, mtot_ref, o_ref
):
    own_live = counts[0] * FT
    tail = mv_ref.shape[0]
    rows = pl.program_id(0) * TQ + lax.broadcasted_iota(jnp.int32, (TQ, 1), 0)
    row_live = rows < own_live
    for h in range(o_ref.shape[1] // HD):
        c = head_cols(h)
        acc_mot = jnp.dot(
            w_ref[:, h * tail : (h + 1) * tail],
            mv_ref[:, c],
            preferred_element_type=jnp.float32,
        )
        top_own = top_ref[:, h : h + 1]
        top_mot = mtop_ref[:, h : h + 1]
        peak = jnp.maximum(top_own, top_mot)
        factor_own = jnp.exp(top_own - peak)
        factor_mot = jnp.exp(top_mot - peak)
        scale = 1.0 / (
            tot_ref[:, h : h + 1] * factor_own + mtot_ref[:, h : h + 1] * factor_mot
        )
        mixed = (acc_ref[:, c] * factor_own + acc_mot * factor_mot) * scale
        o_ref[:, c] = jnp.where(row_live, mixed, 0.0).astype(o_ref.dtype)


def rows_of(width):
    return pl.BlockSpec((TQ, width), lambda i, c: (i, 0))


def whole(rows, width):
    return pl.BlockSpec((rows, width), lambda i, c: (0, 0))


def call(kernel, counts, operands, in_specs, outs, cost):
    span = operands[0].shape[0]
    shapes = [jax.ShapeDtypeStruct((span, w), t) for w, t in outs]
    return pl.pallas_call(
        kernel,
        out_shape=tuple(shapes),
        grid_spec=pltpu.PrefetchScalarGridSpec(
            num_scalar_prefetch=1,
            grid=(span // TQ,),
            in_specs=in_specs,
            out_specs=[rows_of(w) for w, _ in outs],
        ),
        compiler_params=pltpu.CompilerParams(dimension_semantics=("arbitrary",)),
        cost_estimate=cost,
    )(counts, *operands)


def relay_plan(mesh):
    where = [mesh.devices[c, 0, 0].coords for c in range(mesh.devices.shape[0])]
    inner, first, second = [], [], []
    for c in range(1, len(where)):
        (xs, ys, zs), (xr, yr, zr) = where[c - 1], where[c]
        via = [j for j, (x, y, z) in enumerate(where) if y == ys and z == zr]
        if ys == yr or not via:
            inner.append((c - 1, c))
        else:
            first.append((c - 1, via[0]))
            second.append((via[0], c))
    return inner, first, second


def body(plan, queries, keys, values, frames, motion):
    stretch_index = lax.axis_index("stretch")
    tail = MOT_CAP * FT
    count_own = frames[stretch_index]
    counts = jnp.stack([count_own, motion[stretch_index]]).astype(jnp.int32)
    tail_begin = (count_own - MOT_CAP) * FT
    k_heads = lax.all_to_all(keys, "head", split_axis=1, concat_axis=0, tiled=True)
    v_heads = lax.all_to_all(values, "head", split_axis=1, concat_axis=0, tiled=True)
    k_tail = lax.dynamic_slice_in_dim(k_heads, tail_begin, tail, 0)
    v_tail = lax.dynamic_slice_in_dim(v_heads, tail_begin, tail, 0)
    k_prior = from_behind(k_tail, "stretch", 1)
    inner, first, second = plan
    half = tail // 2
    v_near = from_behind(v_tail[:half], "stretch", 1)
    v_far = v_tail[half:]
    if first:
        v_far = lax.ppermute(v_far, "stretch", inner) + lax.ppermute(
            lax.ppermute(v_far, "stretch", first), "stretch", second
        )
    else:
        v_far = from_behind(v_far, "stretch", 1)
    v_prior = jnp.concatenate([v_near, v_far], axis=0)
    q_heads = lax.all_to_all(queries, "head", split_axis=1, concat_axis=0, tiled=True)
    span, local = q_heads.shape
    heads = local // HD
    f32 = jnp.float32
    acc, top, tot = call(
        own_kernel,
        counts,
        (q_heads, k_heads, v_heads),
        [rows_of(local), whole(span, local), whole(span, local)],
        [(local, f32), (COLS, f32), (COLS, f32)],
        pl.CostEstimate(
            flops=heads * 2 * span * span * 3 * HD,
            transcendentals=heads * span * span,
            bytes_accessed=3 * span * local * 2 + span * local * 4,
        ),
    )
    w_mot, mtop, mtot = call(
        mscore_kernel,
        counts,
        (q_heads, k_prior),
        [rows_of(local), whole(tail, local)],
        [(heads * tail, jnp.bfloat16), (COLS, f32), (COLS, f32)],
        pl.CostEstimate(
            flops=heads * 2 * span * tail * 2 * HD,
            transcendentals=heads * span * tail,
            bytes_accessed=span * local * 2 + tail * local * 2 + span * heads * tail * 2,
        ),
    )
    (mixed,) = call(
        merge_kernel,
        counts,
        (w_mot, v_prior, acc, top, tot, mtop, mtot),
        [
            rows_of(heads * tail),
            whole(tail, local),
            rows_of(local),
            rows_of(COLS),
            rows_of(COLS),
            rows_of(COLS),
            rows_of(COLS),
        ],
        [(local, jnp.bfloat16)],
        pl.CostEstimate(
            flops=heads * 2 * span * tail * HD,
            transcendentals=2 * heads * span,
            bytes_accessed=span * heads * tail * 2 + span * local * 6 + tail * local * 2,
        ),
    )
    return lax.all_to_all(mixed, "head", split_axis=0, concat_axis=1, tiled=True)


def solution(mesh):
    placed = (
        P(("cfg", "stretch", "head"), None),
        P(("cfg", "stretch", "head"), None),
        P(("cfg", "stretch", "head"), None),
        P(),
        P(),
    )
    return jax.shard_map(
        functools.partial(body, relay_plan(mesh)),
        mesh=mesh,
        in_specs=placed,
        out_specs=P(("cfg", "stretch", "head"), None),
        check_vma=False,
    )
```

```python
import functools
import math

import jax
import jax.numpy as jnp
from jax import lax
from jax.experimental import pallas as pl
from jax.experimental.pallas import tpu as pltpu
from jax.sharding import PartitionSpec as P

HD = 128
FT = 128
MOT_CAP = 4

NEG = -1e30
TQ = 448
COLS = 8


def from_behind(shard, axis, by):
    size = lax.axis_size(axis)
    pairs = [(i, i + by) for i in range(size) if 0 <= i + by < size]
    return lax.ppermute(shard, axis, pairs)


def scaled_scores(q, k, live):
    scores = lax.dot_general(
        q, k, (((1,), (1,)), ((), ())), preferred_element_type=jnp.float32
    )
    scores = scores * (1.0 / math.sqrt(HD))
    return jnp.where(live, scores, NEG)


def head_cols(h):
    return slice(h * HD, (h + 1) * HD)


def own_kernel(counts, q_ref, k_ref, v_ref, acc_ref, top_ref, tot_ref):
    own_live = counts[0] * FT
    span = k_ref.shape[0]
    key_live = lax.broadcasted_iota(jnp.int32, (1, span), 1) < own_live
    for h in range(acc_ref.shape[1] // HD):
        c = head_cols(h)
        masked = scaled_scores(q_ref[:, c], k_ref[:, c], key_live)
        top = jnp.max(masked, axis=1, keepdims=True)
        weights = jnp.exp(masked - top).astype(jnp.bfloat16)
        v = v_ref[:, c]
        v_ext = jnp.concatenate([v, jnp.ones_like(v)], axis=1)
        both = jnp.dot(weights, v_ext, preferred_element_type=jnp.float32)
        acc_ref[:, c] = both[:, :HD]
        top_ref[:, h : h + 1] = top
        tot_ref[:, h : h + 1] = both[:, HD : HD + 1]


def finish_kernel(
    counts, q_ref, mk_ref, mv_ref, acc_ref, top_ref, tot_ref, o_ref
):
    own_live = counts[0] * FT
    mot_start = (MOT_CAP - counts[1]) * FT
    tail = mk_ref.shape[0]
    slot_live = lax.broadcasted_iota(jnp.int32, (1, tail), 1) >= mot_start
    rows = pl.program_id(0) * TQ + lax.broadcasted_iota(jnp.int32, (TQ, 1), 0)
    row_live = rows < own_live
    for h in range(o_ref.shape[1] // HD):
        c = head_cols(h)
        masked = scaled_scores(q_ref[:, c], mk_ref[:, c], slot_live)
        top_mot = jnp.max(masked, axis=1, keepdims=True)
        weights = jnp.exp(masked - top_mot).astype(jnp.bfloat16)
        mv = mv_ref[:, c]
        mv_ext = jnp.concatenate([mv, jnp.ones_like(mv)], axis=1)
        both = jnp.dot(weights, mv_ext, preferred_element_type=jnp.float32)
        top_own = top_ref[:, h : h + 1]
        peak = jnp.maximum(top_own, top_mot)
        factor_own = jnp.exp(top_own - peak)
        factor_mot = jnp.exp(top_mot - peak)
        scale = 1.0 / (
            tot_ref[:, h : h + 1] * factor_own + both[:, HD : HD + 1] * factor_mot
        )
        mixed = (acc_ref[:, c] * factor_own + both[:, :HD] * factor_mot) * scale
        o_ref[:, c] = jnp.where(row_live, mixed, 0.0).astype(o_ref.dtype)


def rows_of(width):
    return pl.BlockSpec((TQ, width), lambda i, c: (i, 0))


def whole(rows, width):
    return pl.BlockSpec((rows, width), lambda i, c: (0, 0))


def call(kernel, counts, operands, in_specs, outs, cost):
    span = operands[0].shape[0]
    shapes = [jax.ShapeDtypeStruct((span, w), t) for w, t in outs]
    return pl.pallas_call(
        kernel,
        out_shape=tuple(shapes),
        grid_spec=pltpu.PrefetchScalarGridSpec(
            num_scalar_prefetch=1,
            grid=(span // TQ,),
            in_specs=in_specs,
            out_specs=[rows_of(w) for w, _ in outs],
        ),
        compiler_params=pltpu.CompilerParams(dimension_semantics=("arbitrary",)),
        cost_estimate=cost,
    )(counts, *operands)


def relay_plan(mesh):
    where = [mesh.devices[c, 0, 0].coords for c in range(mesh.devices.shape[0])]
    inner, first, second = [], [], []
    for c in range(1, len(where)):
        (xs, ys, zs), (xr, yr, zr) = where[c - 1], where[c]
        via = [j for j, (x, y, z) in enumerate(where) if y == ys and z == zr]
        if ys == yr or not via:
            inner.append((c - 1, c))
        else:
            first.append((c - 1, via[0]))
            second.append((via[0], c))
    return inner, first, second


def body(plan, queries, keys, values, frames, motion):
    stretch_index = lax.axis_index("stretch")
    tail = MOT_CAP * FT
    count_own = frames[stretch_index]
    counts = jnp.stack([count_own, motion[stretch_index]]).astype(jnp.int32)
    tail_begin = (count_own - MOT_CAP) * FT
    k_heads = lax.all_to_all(keys, "head", split_axis=1, concat_axis=0, tiled=True)
    v_heads = lax.all_to_all(values, "head", split_axis=1, concat_axis=0, tiled=True)
    k_tail = lax.dynamic_slice_in_dim(k_heads, tail_begin, tail, 0)
    v_tail = lax.dynamic_slice_in_dim(v_heads, tail_begin, tail, 0)
    k_prior = from_behind(k_tail, "stretch", 1)
    inner, first, second = plan
    half = tail // 2
    v_near = from_behind(v_tail[:half], "stretch", 1)
    v_far = v_tail[half:]
    if first:
        v_far = lax.ppermute(v_far, "stretch", inner) + lax.ppermute(
            lax.ppermute(v_far, "stretch", first), "stretch", second
        )
    else:
        v_far = from_behind(v_far, "stretch", 1)
    v_prior = jnp.concatenate([v_near, v_far], axis=0)
    q_heads = lax.all_to_all(queries, "head", split_axis=1, concat_axis=0, tiled=True)
    span, local = q_heads.shape
    heads = local // HD
    f32 = jnp.float32
    acc, top, tot = call(
        own_kernel,
        counts,
        (q_heads, k_heads, v_heads),
        [rows_of(local), whole(span, local), whole(span, local)],
        [(local, f32), (COLS, f32), (COLS, f32)],
        pl.CostEstimate(
            flops=heads * 2 * span * span * 3 * HD,
            transcendentals=heads * span * span,
            bytes_accessed=3 * span * local * 2 + span * local * 4,
        ),
    )
    (mixed,) = call(
        finish_kernel,
        counts,
        (q_heads, k_prior, v_prior, acc, top, tot),
        [
            rows_of(local),
            whole(tail, local),
            whole(tail, local),
            rows_of(local),
            rows_of(COLS),
            rows_of(COLS),
        ],
        [(local, jnp.bfloat16)],
        pl.CostEstimate(
            flops=heads * 2 * span * tail * 3 * HD,
            transcendentals=heads * span * tail,
            bytes_accessed=span * local * 8 + 2 * tail * local * 2,
        ),
    )
    return lax.all_to_all(mixed, "head", split_axis=0, concat_axis=1, tiled=True)


def solution(mesh):
    placed = (
        P(("cfg", "stretch", "head"), None),
        P(("cfg", "stretch", "head"), None),
        P(("cfg", "stretch", "head"), None),
        P(),
        P(),
    )
    return jax.shard_map(
        functools.partial(body, relay_plan(mesh)),
        mesh=mesh,
        in_specs=placed,
        out_specs=P(("cfg", "stretch", "head"), None),
        check_vma=False,
    )
```

```python
import functools
import math

import jax
import jax.numpy as jnp
from jax import lax
from jax.experimental import pallas as pl
from jax.experimental.pallas import tpu as pltpu
from jax.sharding import PartitionSpec as P

HD = 128
FT = 128
MOT_CAP = 4

NEG = -1e30
TQ = 448
COLS = 8


def from_behind(shard, axis, by):
    size = lax.axis_size(axis)
    pairs = [(i, i + by) for i in range(size) if 0 <= i + by < size]
    return lax.ppermute(shard, axis, pairs)


def scaled_scores(q, k, live):
    scores = lax.dot_general(
        q, k, (((1,), (1,)), ((), ())), preferred_element_type=jnp.float32
    )
    scores = scores * (1.0 / math.sqrt(HD))
    return jnp.where(live, scores, NEG)


def head_cols(h):
    return slice(h * HD, (h + 1) * HD)


def own_kernel(counts, q_ref, k_ref, v_ref, acc_ref, top_ref, tot_ref):
    own_live = counts[0] * FT
    span = k_ref.shape[0]
    key_live = lax.broadcasted_iota(jnp.int32, (1, span), 1) < own_live
    for h in range(acc_ref.shape[1] // HD):
        c = head_cols(h)
        masked = scaled_scores(q_ref[:, c], k_ref[:, c], key_live)
        top = jnp.max(masked, axis=1, keepdims=True)
        weights = jnp.exp(masked - top).astype(jnp.bfloat16)
        v = v_ref[:, c]
        v_ext = jnp.concatenate([v, jnp.ones_like(v)], axis=1)
        both = jnp.dot(weights, v_ext, preferred_element_type=jnp.float32)
        acc_ref[:, c] = both[:, :HD]
        top_ref[:, h : h + 1] = top
        tot_ref[:, h : h + 1] = both[:, HD : HD + 1]


def mscore_kernel(counts, q_ref, mk_ref, w_ref, top_ref, tot_ref):
    mot_start = (MOT_CAP - counts[1]) * FT
    tail = mk_ref.shape[0]
    slot_live = lax.broadcasted_iota(jnp.int32, (1, tail), 1) >= mot_start
    ones = jnp.ones((tail, HD), jnp.bfloat16)
    for h in range(q_ref.shape[1] // HD):
        c = head_cols(h)
        masked = scaled_scores(q_ref[:, c], mk_ref[:, c], slot_live)
        top = jnp.max(masked, axis=1, keepdims=True)
        weights = jnp.exp(masked - top).astype(jnp.bfloat16)
        w_ref[:, h * tail : (h + 1) * tail] = weights
        total = jnp.dot(weights, ones, preferred_element_type=jnp.float32)
        top_ref[:, h : h + 1] = top
        tot_ref[:, h : h + 1] = total[:, 0:1]


def merge_kernel(
    counts, w_ref, mv_ref, acc_ref, top_ref, tot_ref, mtop_ref, mtot_ref, o_ref
):
    own_live = counts[0] * FT
    tail = mv_ref.shape[0]
    rows = pl.program_id(0) * TQ + lax.broadcasted_iota(jnp.int32, (TQ, 1), 0)
    row_live = rows < own_live
    for h in range(o_ref.shape[1] // HD):
        c = head_cols(h)
        acc_mot = jnp.dot(
            w_ref[:, h * tail : (h + 1) * tail],
            mv_ref[:, c],
            preferred_element_type=jnp.float32,
        )
        top_own = top_ref[:, h : h + 1]
        top_mot = mtop_ref[:, h : h + 1]
        peak = jnp.maximum(top_own, top_mot)
        factor_own = jnp.exp(top_own - peak)
        factor_mot = jnp.exp(top_mot - peak)
        scale = 1.0 / (
            tot_ref[:, h : h + 1] * factor_own + mtot_ref[:, h : h + 1] * factor_mot
        )
        mixed = (acc_ref[:, c] * factor_own + acc_mot * factor_mot) * scale
        o_ref[:, c] = jnp.where(row_live, mixed, 0.0).astype(o_ref.dtype)


def rows_of(width):
    return pl.BlockSpec((TQ, width), lambda i, c: (i, 0))


def whole(rows, width):
    return pl.BlockSpec((rows, width), lambda i, c: (0, 0))


def call(kernel, counts, operands, in_specs, outs, cost):
    span = operands[0].shape[0]
    shapes = [jax.ShapeDtypeStruct((span, w), t) for w, t in outs]
    return pl.pallas_call(
        kernel,
        out_shape=tuple(shapes),
        grid_spec=pltpu.PrefetchScalarGridSpec(
            num_scalar_prefetch=1,
            grid=(span // TQ,),
            in_specs=in_specs,
            out_specs=[rows_of(w) for w, _ in outs],
        ),
        compiler_params=pltpu.CompilerParams(dimension_semantics=("arbitrary",)),
        cost_estimate=cost,
    )(counts, *operands)


def relay_plan(mesh):
    where = [mesh.devices[c, 0, 0].coords for c in range(mesh.devices.shape[0])]
    inner, first, second = [], [], []
    for c in range(1, len(where)):
        (xs, ys, zs), (xr, yr, zr) = where[c - 1], where[c]
        via = [j for j, (x, y, z) in enumerate(where) if y == ys and z == zr]
        if ys == yr or not via:
            inner.append((c - 1, c))
        else:
            first.append((c - 1, via[0]))
            second.append((via[0], c))
    return inner, first, second


def body(plan, queries, keys, values, frames, motion):
    stretch_index = lax.axis_index("stretch")
    tail = MOT_CAP * FT
    count_own = frames[stretch_index]
    counts = jnp.stack([count_own, motion[stretch_index]]).astype(jnp.int32)
    tail_begin = (count_own - MOT_CAP) * FT
    groups = lax.axis_size("head")
    rows, width = keys.shape
    local = width // groups

    def by_target(x):
        return x.reshape(rows, groups, local).transpose(1, 0, 2)

    kv_send = jnp.stack([by_target(keys), by_target(values)], axis=1)
    kv_recv = lax.all_to_all(kv_send, "head", split_axis=0, concat_axis=0, tiled=True)
    kv_rows = kv_recv.transpose(1, 0, 2, 3).reshape(2, groups * rows, local)
    k_heads, v_heads = kv_rows[0], kv_rows[1]
    k_tail = lax.dynamic_slice_in_dim(k_heads, tail_begin, tail, 0)
    v_tail = lax.dynamic_slice_in_dim(v_heads, tail_begin, tail, 0)
    k_prior = from_behind(k_tail, "stretch", 1)
    inner, first, second = plan
    half = tail // 2
    v_near = from_behind(v_tail[:half], "stretch", 1)
    v_far = v_tail[half:]
    if first:
        v_far = lax.ppermute(v_far, "stretch", inner) + lax.ppermute(
            lax.ppermute(v_far, "stretch", first), "stretch", second
        )
    else:
        v_far = from_behind(v_far, "stretch", 1)
    v_prior = jnp.concatenate([v_near, v_far], axis=0)
    q_heads = lax.all_to_all(queries, "head", split_axis=1, concat_axis=0, tiled=True)
    span, local = q_heads.shape
    heads = local // HD
    f32 = jnp.float32
    acc, top, tot = call(
        own_kernel,
        counts,
        (q_heads, k_heads, v_heads),
        [rows_of(local), whole(span, local), whole(span, local)],
        [(local, f32), (COLS, f32), (COLS, f32)],
        pl.CostEstimate(
            flops=heads * 2 * span * span * 3 * HD,
            transcendentals=heads * span * span,
            bytes_accessed=3 * span * local * 2 + span * local * 4,
        ),
    )
    w_mot, mtop, mtot = call(
        mscore_kernel,
        counts,
        (q_heads, k_prior),
        [rows_of(local), whole(tail, local)],
        [(heads * tail, jnp.bfloat16), (COLS, f32), (COLS, f32)],
        pl.CostEstimate(
            flops=heads * 2 * span * tail * 2 * HD,
            transcendentals=heads * span * tail,
            bytes_accessed=span * local * 2 + tail * local * 2 + span * heads * tail * 2,
        ),
    )
    (mixed,) = call(
        merge_kernel,
        counts,
        (w_mot, v_prior, acc, top, tot, mtop, mtot),
        [
            rows_of(heads * tail),
            whole(tail, local),
            rows_of(local),
            rows_of(COLS),
            rows_of(COLS),
            rows_of(COLS),
            rows_of(COLS),
        ],
        [(local, jnp.bfloat16)],
        pl.CostEstimate(
            flops=heads * 2 * span * tail * HD,
            transcendentals=2 * heads * span,
            bytes_accessed=span * heads * tail * 2 + span * local * 6 + tail * local * 2,
        ),
    )
    return lax.all_to_all(mixed, "head", split_axis=0, concat_axis=1, tiled=True)


def solution(mesh):
    placed = (
        P(("cfg", "stretch", "head"), None),
        P(("cfg", "stretch", "head"), None),
        P(("cfg", "stretch", "head"), None),
        P(),
        P(),
    )
    return jax.shard_map(
        functools.partial(body, relay_plan(mesh)),
        mesh=mesh,
        in_specs=placed,
        out_specs=P(("cfg", "stretch", "head"), None),
        check_vma=False,
    )
```

```python
import functools
import math

import jax
import jax.numpy as jnp
from jax import lax
from jax.experimental import pallas as pl
from jax.experimental.pallas import tpu as pltpu
from jax.sharding import PartitionSpec as P

HD = 128
FT = 128
MOT_CAP = 4

NEG = -1e30
TQ = 448
COLS = 8


def from_behind(shard, axis, by):
    size = lax.axis_size(axis)
    pairs = [(i, i + by) for i in range(size) if 0 <= i + by < size]
    return lax.ppermute(shard, axis, pairs)


def scaled_scores(q, k, live):
    scores = lax.dot_general(
        q, k, (((1,), (1,)), ((), ())), preferred_element_type=jnp.float32
    )
    scores = scores * (1.0 / math.sqrt(HD))
    return jnp.where(live, scores, NEG)


def head_cols(h):
    return slice(h * HD, (h + 1) * HD)


def own_kernel(counts, q_ref, k_ref, v_ref, acc_ref, top_ref, tot_ref):
    own_live = counts[0] * FT
    span = k_ref.shape[0]
    key_live = lax.broadcasted_iota(jnp.int32, (1, span), 1) < own_live
    for h in range(acc_ref.shape[1] // HD):
        c = head_cols(h)
        masked = scaled_scores(q_ref[:, c], k_ref[:, c], key_live)
        top = jnp.max(masked, axis=1, keepdims=True)
        weights = jnp.exp(masked - top).astype(jnp.bfloat16)
        v = v_ref[:, c]
        v_ext = jnp.concatenate([v, jnp.ones_like(v)], axis=1)
        both = jnp.dot(weights, v_ext, preferred_element_type=jnp.float32)
        acc_ref[:, c] = both[:, :HD]
        top_ref[:, h : h + 1] = top
        tot_ref[:, h : h + 1] = both[:, HD : HD + 1]


def mscore_kernel(counts, q_ref, mk_ref, w_ref, top_ref, tot_ref):
    mot_start = (MOT_CAP - counts[1]) * FT
    tail = mk_ref.shape[0]
    slot_live = lax.broadcasted_iota(jnp.int32, (1, tail), 1) >= mot_start
    ones = jnp.ones((tail, HD), jnp.bfloat16)
    for h in range(q_ref.shape[1] // HD):
        c = head_cols(h)
        masked = scaled_scores(q_ref[:, c], mk_ref[:, c], slot_live)
        top = jnp.max(masked, axis=1, keepdims=True)
        weights = jnp.exp(masked - top).astype(jnp.bfloat16)
        w_ref[:, h * tail : (h + 1) * tail] = weights
        total = jnp.dot(weights, ones, preferred_element_type=jnp.float32)
        top_ref[:, h : h + 1] = top
        tot_ref[:, h : h + 1] = total[:, 0:1]


def merge_kernel(
    counts, w_ref, mv_ref, acc_ref, top_ref, tot_ref, mtop_ref, mtot_ref, o_ref
):
    own_live = counts[0] * FT
    tail = mv_ref.shape[0]
    rows = pl.program_id(0) * TQ + lax.broadcasted_iota(jnp.int32, (TQ, 1), 0)
    row_live = rows < own_live
    for h in range(o_ref.shape[1] // HD):
        c = head_cols(h)
        acc_mot = jnp.dot(
            w_ref[:, h * tail : (h + 1) * tail],
            mv_ref[:, c],
            preferred_element_type=jnp.float32,
        )
        top_own = top_ref[:, h : h + 1]
        top_mot = mtop_ref[:, h : h + 1]
        peak = jnp.maximum(top_own, top_mot)
        factor_own = jnp.exp(top_own - peak)
        factor_mot = jnp.exp(top_mot - peak)
        scale = 1.0 / (
            tot_ref[:, h : h + 1] * factor_own + mtot_ref[:, h : h + 1] * factor_mot
        )
        mixed = (acc_ref[:, c] * factor_own + acc_mot * factor_mot) * scale
        o_ref[:, c] = jnp.where(row_live, mixed, 0.0).astype(o_ref.dtype)


def rows_of(width):
    return pl.BlockSpec((TQ, width), lambda i, c: (i, 0))


def whole(rows, width):
    return pl.BlockSpec((rows, width), lambda i, c: (0, 0))


def call(kernel, counts, operands, in_specs, outs, cost):
    span = operands[0].shape[0]
    shapes = [jax.ShapeDtypeStruct((span, w), t) for w, t in outs]
    return pl.pallas_call(
        kernel,
        out_shape=tuple(shapes),
        grid_spec=pltpu.PrefetchScalarGridSpec(
            num_scalar_prefetch=1,
            grid=(span // TQ,),
            in_specs=in_specs,
            out_specs=[rows_of(w) for w, _ in outs],
        ),
        compiler_params=pltpu.CompilerParams(dimension_semantics=("arbitrary",)),
        cost_estimate=cost,
    )(counts, *operands)


def relay_plan(mesh):
    where = [mesh.devices[c, 0, 0].coords for c in range(mesh.devices.shape[0])]
    inner, first, second = [], [], []
    for c in range(1, len(where)):
        (xs, ys, zs), (xr, yr, zr) = where[c - 1], where[c]
        via = [j for j, (x, y, z) in enumerate(where) if y == ys and z == zr]
        if ys == yr or not via:
            inner.append((c - 1, c))
        else:
            first.append((c - 1, via[0]))
            second.append((via[0], c))
    return inner, first, second


def body(plan, queries, keys, values, frames, motion):
    stretch_index = lax.axis_index("stretch")
    tail = MOT_CAP * FT
    count_own = frames[stretch_index]
    counts = jnp.stack([count_own, motion[stretch_index]]).astype(jnp.int32)
    tail_begin = (count_own - MOT_CAP) * FT
    groups = lax.axis_size("head")
    rows, width = keys.shape
    local = width // groups

    def by_target(x):
        return x.reshape(rows, groups, local).transpose(1, 0, 2)

    kv_send = jnp.stack([by_target(keys), by_target(values)], axis=1)
    kv_recv = lax.all_to_all(kv_send, "head", split_axis=0, concat_axis=0, tiled=True)
    kv_rows = kv_recv.transpose(1, 0, 2, 3).reshape(2, groups * rows, local)
    k_heads, v_heads = kv_rows[0], kv_rows[1]
    k_tail = lax.dynamic_slice_in_dim(k_heads, tail_begin, tail, 0)
    v_tail = lax.dynamic_slice_in_dim(v_heads, tail_begin, tail, 0)
    k_prior = from_behind(k_tail, "stretch", 1)
    inner, first, second = plan
    if first:
        v_prior = lax.ppermute(v_tail, "stretch", inner) + lax.ppermute(
            lax.ppermute(v_tail, "stretch", first), "stretch", second
        )
    else:
        v_prior = from_behind(v_tail, "stretch", 1)
    q_heads = lax.all_to_all(queries, "head", split_axis=1, concat_axis=0, tiled=True)
    span, local = q_heads.shape
    heads = local // HD
    f32 = jnp.float32
    acc, top, tot = call(
        own_kernel,
        counts,
        (q_heads, k_heads, v_heads),
        [rows_of(local), whole(span, local), whole(span, local)],
        [(local, f32), (COLS, f32), (COLS, f32)],
        pl.CostEstimate(
            flops=heads * 2 * span * span * 3 * HD,
            transcendentals=heads * span * span,
            bytes_accessed=3 * span * local * 2 + span * local * 4,
        ),
    )
    w_mot, mtop, mtot = call(
        mscore_kernel,
        counts,
        (q_heads, k_prior),
        [rows_of(local), whole(tail, local)],
        [(heads * tail, jnp.bfloat16), (COLS, f32), (COLS, f32)],
        pl.CostEstimate(
            flops=heads * 2 * span * tail * 2 * HD,
            transcendentals=heads * span * tail,
            bytes_accessed=span * local * 2 + tail * local * 2 + span * heads * tail * 2,
        ),
    )
    (mixed,) = call(
        merge_kernel,
        counts,
        (w_mot, v_prior, acc, top, tot, mtop, mtot),
        [
            rows_of(heads * tail),
            whole(tail, local),
            rows_of(local),
            rows_of(COLS),
            rows_of(COLS),
            rows_of(COLS),
            rows_of(COLS),
        ],
        [(local, jnp.bfloat16)],
        pl.CostEstimate(
            flops=heads * 2 * span * tail * HD,
            transcendentals=2 * heads * span,
            bytes_accessed=span * heads * tail * 2 + span * local * 6 + tail * local * 2,
        ),
    )
    return lax.all_to_all(mixed, "head", split_axis=0, concat_axis=1, tiled=True)


def solution(mesh):
    placed = (
        P(("cfg", "stretch", "head"), None),
        P(("cfg", "stretch", "head"), None),
        P(("cfg", "stretch", "head"), None),
        P(),
        P(),
    )
    return jax.shard_map(
        functools.partial(body, relay_plan(mesh)),
        mesh=mesh,
        in_specs=placed,
        out_specs=P(("cfg", "stretch", "head"), None),
        check_vma=False,
    )
```

```python
import functools
import math

import jax
import jax.numpy as jnp
from jax import lax
from jax.experimental import pallas as pl
from jax.experimental.pallas import tpu as pltpu
from jax.sharding import PartitionSpec as P

HD = 128
FT = 128
MOT_CAP = 4

NEG = -1e30
TQ = 448
MT = 224
COLS = 8


def from_behind(shard, axis, by):
    size = lax.axis_size(axis)
    pairs = [(i, i + by) for i in range(size) if 0 <= i + by < size]
    return lax.ppermute(shard, axis, pairs)


def scaled_scores(q, k, live):
    scores = lax.dot_general(
        q, k, (((1,), (1,)), ((), ())), preferred_element_type=jnp.float32
    )
    scores = scores * (1.0 / math.sqrt(HD))
    return jnp.where(live, scores, NEG)


def head_cols(h):
    return slice(h * HD, (h + 1) * HD)


def own_kernel(counts, q_ref, k_ref, v_ref, acc_ref, top_ref, tot_ref):
    own_live = counts[0] * FT
    span = k_ref.shape[0]
    key_live = lax.broadcasted_iota(jnp.int32, (1, span), 1) < own_live
    for h in range(acc_ref.shape[1] // HD):
        c = head_cols(h)
        masked = scaled_scores(q_ref[:, c], k_ref[:, c], key_live)
        top = jnp.max(masked, axis=1, keepdims=True)
        weights = jnp.exp(masked - top).astype(jnp.bfloat16)
        v = v_ref[:, c]
        v_ext = jnp.concatenate([v, jnp.ones_like(v)], axis=1)
        both = jnp.dot(weights, v_ext, preferred_element_type=jnp.float32)
        acc_ref[:, c] = both[:, :HD]
        top_ref[:, h : h + 1] = top
        tot_ref[:, h : h + 1] = both[:, HD : HD + 1]


def mscore_kernel(counts, q_ref, mk_ref, w_ref, top_ref, tot_ref):
    mot_start = (MOT_CAP - counts[1]) * FT
    tail = mk_ref.shape[0]
    slot_live = lax.broadcasted_iota(jnp.int32, (1, tail), 1) >= mot_start
    ones = jnp.ones((tail, HD), jnp.bfloat16)
    for h in range(q_ref.shape[1] // HD):
        c = head_cols(h)
        masked = scaled_scores(q_ref[:, c], mk_ref[:, c], slot_live)
        top = jnp.max(masked, axis=1, keepdims=True)
        weights = jnp.exp(masked - top).astype(jnp.bfloat16)
        w_ref[:, h * tail : (h + 1) * tail] = weights
        total = jnp.dot(weights, ones, preferred_element_type=jnp.float32)
        top_ref[:, h : h + 1] = top
        tot_ref[:, h : h + 1] = total[:, 0:1]


def merge_kernel(
    counts, w_ref, mv_ref, acc_ref, top_ref, tot_ref, mtop_ref, mtot_ref, o_ref
):
    own_live = counts[0] * FT
    tail = mv_ref.shape[0]
    tq = o_ref.shape[0]
    rows = pl.program_id(0) * tq + lax.broadcasted_iota(jnp.int32, (tq, 1), 0)
    row_live = rows < own_live
    for h in range(o_ref.shape[1] // HD):
        c = head_cols(h)
        acc_mot = jnp.dot(
            w_ref[:, h * tail : (h + 1) * tail],
            mv_ref[:, c],
            preferred_element_type=jnp.float32,
        )
        top_own = top_ref[:, h : h + 1]
        top_mot = mtop_ref[:, h : h + 1]
        peak = jnp.maximum(top_own, top_mot)
        factor_own = jnp.exp(top_own - peak)
        factor_mot = jnp.exp(top_mot - peak)
        scale = 1.0 / (
            tot_ref[:, h : h + 1] * factor_own + mtot_ref[:, h : h + 1] * factor_mot
        )
        mixed = (acc_ref[:, c] * factor_own + acc_mot * factor_mot) * scale
        o_ref[:, c] = jnp.where(row_live, mixed, 0.0).astype(o_ref.dtype)


def rows_of(width, tq=TQ):
    return pl.BlockSpec((tq, width), lambda i, c: (i, 0))


def whole(rows, width):
    return pl.BlockSpec((rows, width), lambda i, c: (0, 0))


def call(kernel, counts, operands, in_specs, outs, cost, tq=TQ):
    span = operands[0].shape[0]
    shapes = [jax.ShapeDtypeStruct((span, w), t) for w, t in outs]
    return pl.pallas_call(
        kernel,
        out_shape=tuple(shapes),
        grid_spec=pltpu.PrefetchScalarGridSpec(
            num_scalar_prefetch=1,
            grid=(span // tq,),
            in_specs=in_specs,
            out_specs=[rows_of(w, tq) for w, _ in outs],
        ),
        compiler_params=pltpu.CompilerParams(dimension_semantics=("arbitrary",)),
        cost_estimate=cost,
    )(counts, *operands)


def relay_plan(mesh):
    where = [mesh.devices[c, 0, 0].coords for c in range(mesh.devices.shape[0])]
    inner, first, second = [], [], []
    for c in range(1, len(where)):
        (xs, ys, zs), (xr, yr, zr) = where[c - 1], where[c]
        via = [j for j, (x, y, z) in enumerate(where) if y == ys and z == zr]
        if ys == yr or not via:
            inner.append((c - 1, c))
        else:
            first.append((c - 1, via[0]))
            second.append((via[0], c))
    return inner, first, second


def body(plan, queries, keys, values, frames, motion):
    stretch_index = lax.axis_index("stretch")
    tail = MOT_CAP * FT
    count_own = frames[stretch_index]
    counts = jnp.stack([count_own, motion[stretch_index]]).astype(jnp.int32)
    tail_begin = (count_own - MOT_CAP) * FT
    groups = lax.axis_size("head")
    rows, width = keys.shape
    local = width // groups

    def by_target(x):
        return x.reshape(rows, groups, local).transpose(1, 0, 2)

    kv_send = jnp.stack([by_target(keys), by_target(values)], axis=1)
    kv_recv = lax.all_to_all(kv_send, "head", split_axis=0, concat_axis=0, tiled=True)
    kv_rows = kv_recv.transpose(1, 0, 2, 3).reshape(2, groups * rows, local)
    k_heads, v_heads = kv_rows[0], kv_rows[1]
    kv_tail = lax.dynamic_slice_in_dim(kv_rows, tail_begin, tail, 1)
    inner, first, second = plan
    half = tail // 2
    direct = jnp.concatenate([kv_tail[0], kv_tail[1, :half]], axis=0)
    direct_prior = from_behind(direct, "stretch", 1)
    v_far = kv_tail[1, half:]
    if first:
        v_far = lax.ppermute(v_far, "stretch", inner) + lax.ppermute(
            lax.ppermute(v_far, "stretch", first), "stretch", second
        )
    else:
        v_far = from_behind(v_far, "stretch", 1)
    v_prior = jnp.concatenate([direct_prior[tail:], v_far], axis=0)
    q_heads = lax.all_to_all(queries, "head", split_axis=1, concat_axis=0, tiled=True)
    span, local = q_heads.shape
    heads = local // HD
    f32 = jnp.float32
    acc, top, tot = call(
        own_kernel,
        counts,
        (q_heads, k_heads, v_heads),
        [rows_of(local), whole(span, local), whole(span, local)],
        [(local, f32), (COLS, f32), (COLS, f32)],
        pl.CostEstimate(
            flops=heads * 2 * span * span * 3 * HD,
            transcendentals=heads * span * span,
            bytes_accessed=3 * span * local * 2 + span * local * 4,
        ),
    )
    w_mot, mtop, mtot = call(
        mscore_kernel,
        counts,
        (q_heads, direct_prior),
        [rows_of(local, MT), whole(tail, local)],
        [(heads * tail, jnp.bfloat16), (COLS, f32), (COLS, f32)],
        pl.CostEstimate(
            flops=heads * 2 * span * tail * 2 * HD,
            transcendentals=heads * span * tail,
            bytes_accessed=span * local * 2 + tail * local * 2 + span * heads * tail * 2,
        ),
        tq=MT,
    )
    (mixed,) = call(
        merge_kernel,
        counts,
        (w_mot, v_prior, acc, top, tot, mtop, mtot),
        [
            rows_of(heads * tail, MT),
            whole(tail, local),
            rows_of(local, MT),
            rows_of(COLS, MT),
            rows_of(COLS, MT),
            rows_of(COLS, MT),
            rows_of(COLS, MT),
        ],
        [(local, jnp.bfloat16)],
        pl.CostEstimate(
            flops=heads * 2 * span * tail * HD,
            transcendentals=2 * heads * span,
            bytes_accessed=span * heads * tail * 2 + span * local * 6 + tail * local * 2,
        ),
        tq=MT,
    )
    return lax.all_to_all(mixed, "head", split_axis=0, concat_axis=1, tiled=True)


def solution(mesh):
    placed = (
        P(("cfg", "stretch", "head"), None),
        P(("cfg", "stretch", "head"), None),
        P(("cfg", "stretch", "head"), None),
        P(),
        P(),
    )
    return jax.shard_map(
        functools.partial(body, relay_plan(mesh)),
        mesh=mesh,
        in_specs=placed,
        out_specs=P(("cfg", "stretch", "head"), None),
        check_vma=False,
    )
```

```python
import functools
import math

import jax
import jax.numpy as jnp
from jax import lax
from jax.experimental import pallas as pl
from jax.experimental.pallas import tpu as pltpu
from jax.sharding import PartitionSpec as P

HD = 128
FT = 128
MOT_CAP = 4

NEG = -1e30
TQ = 448
COLS = 8


def from_behind(shard, axis, by):
    size = lax.axis_size(axis)
    pairs = [(i, i + by) for i in range(size) if 0 <= i + by < size]
    return lax.ppermute(shard, axis, pairs)


def scaled_scores(q, k, live):
    scores = lax.dot_general(
        q, k, (((1,), (1,)), ((), ())), preferred_element_type=jnp.float32
    )
    scores = scores * (1.0 / math.sqrt(HD))
    return jnp.where(live, scores, NEG)


def head_cols(h):
    return slice(h * HD, (h + 1) * HD)


def own_kernel(counts, q_ref, k_ref, v_ref, order_ref, acc_ref, top_ref, tot_ref):
    own_live = counts[0] * FT
    span = k_ref.shape[0]
    key_live = lax.broadcasted_iota(jnp.int32, (1, span), 1) < own_live
    for h in range(acc_ref.shape[1] // HD):
        c = head_cols(h)
        masked = scaled_scores(q_ref[:, c], k_ref[:, c], key_live)
        top = jnp.max(masked, axis=1, keepdims=True)
        weights = jnp.exp(masked - top).astype(jnp.bfloat16)
        v = v_ref[:, c]
        v_ext = jnp.concatenate([v, jnp.ones_like(v)], axis=1)
        both = jnp.dot(weights, v_ext, preferred_element_type=jnp.float32)
        acc_ref[:, c] = both[:, :HD]
        top_ref[:, h : h + 1] = top
        tot_ref[:, h : h + 1] = both[:, HD : HD + 1]


def mscore_kernel(counts, q_ref, mk_ref, w_ref, top_ref, tot_ref):
    mot_start = (MOT_CAP - counts[1]) * FT
    tail = mk_ref.shape[0]
    slot_live = lax.broadcasted_iota(jnp.int32, (1, tail), 1) >= mot_start
    ones = jnp.ones((tail, HD), jnp.bfloat16)
    for h in range(q_ref.shape[1] // HD):
        c = head_cols(h)
        masked = scaled_scores(q_ref[:, c], mk_ref[:, c], slot_live)
        top = jnp.max(masked, axis=1, keepdims=True)
        weights = jnp.exp(masked - top).astype(jnp.bfloat16)
        w_ref[:, h * tail : (h + 1) * tail] = weights
        total = jnp.dot(weights, ones, preferred_element_type=jnp.float32)
        top_ref[:, h : h + 1] = top
        tot_ref[:, h : h + 1] = total[:, 0:1]


def merge_kernel(
    counts, w_ref, mv_ref, acc_ref, top_ref, tot_ref, mtop_ref, mtot_ref, o_ref
):
    own_live = counts[0] * FT
    tail = mv_ref.shape[0]
    rows = pl.program_id(0) * TQ + lax.broadcasted_iota(jnp.int32, (TQ, 1), 0)
    row_live = rows < own_live
    for h in range(o_ref.shape[1] // HD):
        c = head_cols(h)
        acc_mot = jnp.dot(
            w_ref[:, h * tail : (h + 1) * tail],
            mv_ref[:, c],
            preferred_element_type=jnp.float32,
        )
        top_own = top_ref[:, h : h + 1]
        top_mot = mtop_ref[:, h : h + 1]
        peak = jnp.maximum(top_own, top_mot)
        factor_own = jnp.exp(top_own - peak)
        factor_mot = jnp.exp(top_mot - peak)
        scale = 1.0 / (
            tot_ref[:, h : h + 1] * factor_own + mtot_ref[:, h : h + 1] * factor_mot
        )
        mixed = (acc_ref[:, c] * factor_own + acc_mot * factor_mot) * scale
        o_ref[:, c] = jnp.where(row_live, mixed, 0.0).astype(o_ref.dtype)


def rows_of(width):
    return pl.BlockSpec((TQ, width), lambda i, c: (i, 0))


def whole(rows, width):
    return pl.BlockSpec((rows, width), lambda i, c: (0, 0))


def call(kernel, counts, operands, in_specs, outs, cost):
    span = operands[0].shape[0]
    shapes = [jax.ShapeDtypeStruct((span, w), t) for w, t in outs]
    return pl.pallas_call(
        kernel,
        out_shape=tuple(shapes),
        grid_spec=pltpu.PrefetchScalarGridSpec(
            num_scalar_prefetch=1,
            grid=(span // TQ,),
            in_specs=in_specs,
            out_specs=[rows_of(w) for w, _ in outs],
        ),
        compiler_params=pltpu.CompilerParams(dimension_semantics=("arbitrary",)),
        cost_estimate=cost,
    )(counts, *operands)


def relay_plan(mesh):
    where = [mesh.devices[c, 0, 0].coords for c in range(mesh.devices.shape[0])]
    inner, first, second = [], [], []
    for c in range(1, len(where)):
        (xs, ys, zs), (xr, yr, zr) = where[c - 1], where[c]
        via = [j for j, (x, y, z) in enumerate(where) if y == ys and z == zr]
        if ys == yr or not via:
            inner.append((c - 1, c))
        else:
            first.append((c - 1, via[0]))
            second.append((via[0], c))
    return inner, first, second


def body(plan, queries, keys, values, frames, motion):
    stretch_index = lax.axis_index("stretch")
    tail = MOT_CAP * FT
    count_own = frames[stretch_index]
    counts = jnp.stack([count_own, motion[stretch_index]]).astype(jnp.int32)
    tail_begin = (count_own - MOT_CAP) * FT
    groups = lax.axis_size("head")
    rows, width = keys.shape
    local = width // groups

    def by_target(x):
        return x.reshape(rows, groups, local).transpose(1, 0, 2)

    kv_send = jnp.stack([by_target(keys), by_target(values)], axis=1)
    kv_recv = lax.all_to_all(kv_send, "head", split_axis=0, concat_axis=0, tiled=True)
    kv_rows = kv_recv.transpose(1, 0, 2, 3).reshape(2, groups * rows, local)
    k_heads, v_heads = kv_rows[0], kv_rows[1]
    k_tail = lax.dynamic_slice_in_dim(k_heads, tail_begin, tail, 0)
    v_tail = lax.dynamic_slice_in_dim(v_heads, tail_begin, tail, 0)
    k_prior = from_behind(k_tail, "stretch", 1)
    inner, first, second = plan
    half = tail // 2
    v_near, k_prior = lax.optimization_barrier((v_tail[:half], k_prior))
    v_near = from_behind(v_near, "stretch", 1)
    v_far = v_tail[half:]
    if first:
        v_far = lax.ppermute(v_far, "stretch", inner) + lax.ppermute(
            lax.ppermute(v_far, "stretch", first), "stretch", second
        )
    else:
        v_far = from_behind(v_far, "stretch", 1)
    v_prior = jnp.concatenate([v_near, v_far], axis=0)
    q_heads = lax.all_to_all(queries, "head", split_axis=1, concat_axis=0, tiled=True)
    span, local = q_heads.shape
    heads = local // HD
    f32 = jnp.float32
    acc, top, tot = call(
        own_kernel,
        counts,
        (q_heads, k_heads, v_heads, k_prior),
        [
            rows_of(local),
            whole(span, local),
            whole(span, local),
            pl.BlockSpec(memory_space=pl.ANY),
        ],
        [(local, f32), (COLS, f32), (COLS, f32)],
        pl.CostEstimate(
            flops=heads * 2 * span * span * 3 * HD,
            transcendentals=heads * span * span,
            bytes_accessed=3 * span * local * 2 + span * local * 4,
        ),
    )
    w_mot, mtop, mtot = call(
        mscore_kernel,
        counts,
        (q_heads, k_prior),
        [rows_of(local), whole(tail, local)],
        [(heads * tail, jnp.bfloat16), (COLS, f32), (COLS, f32)],
        pl.CostEstimate(
            flops=heads * 2 * span * tail * 2 * HD,
            transcendentals=heads * span * tail,
            bytes_accessed=span * local * 2 + tail * local * 2 + span * heads * tail * 2,
        ),
    )
    (mixed,) = call(
        merge_kernel,
        counts,
        (w_mot, v_prior, acc, top, tot, mtop, mtot),
        [
            rows_of(heads * tail),
            whole(tail, local),
            rows_of(local),
            rows_of(COLS),
            rows_of(COLS),
            rows_of(COLS),
            rows_of(COLS),
        ],
        [(local, jnp.bfloat16)],
        pl.CostEstimate(
            flops=heads * 2 * span * tail * HD,
            transcendentals=2 * heads * span,
            bytes_accessed=span * heads * tail * 2 + span * local * 6 + tail * local * 2,
        ),
    )
    return lax.all_to_all(mixed, "head", split_axis=0, concat_axis=1, tiled=True)


def solution(mesh):
    placed = (
        P(("cfg", "stretch", "head"), None),
        P(("cfg", "stretch", "head"), None),
        P(("cfg", "stretch", "head"), None),
        P(),
        P(),
    )
    return jax.shard_map(
        functools.partial(body, relay_plan(mesh)),
        mesh=mesh,
        in_specs=placed,
        out_specs=P(("cfg", "stretch", "head"), None),
        check_vma=False,
    )
```

```python
import functools
import math

import jax
import jax.numpy as jnp
from jax import lax
from jax.experimental import pallas as pl
from jax.experimental.pallas import tpu as pltpu
from jax.sharding import PartitionSpec as P

HD = 128
FT = 128
MOT_CAP = 4

NEG = -1e30
TQ = 448
COLS = 8


def from_behind(shard, axis, by):
    size = lax.axis_size(axis)
    pairs = [(i, i + by) for i in range(size) if 0 <= i + by < size]
    return lax.ppermute(shard, axis, pairs)


def scaled_scores(q, k, live):
    scores = lax.dot_general(
        q, k, (((1,), (1,)), ((), ())), preferred_element_type=jnp.float32
    )
    scores = scores * (1.0 / math.sqrt(HD))
    return jnp.where(live, scores, NEG)


def head_cols(h):
    return slice(h * HD, (h + 1) * HD)


def own_kernel(counts, q_ref, k_ref, v_ref, acc_ref, top_ref, tot_ref):
    own_live = counts[0] * FT
    span = k_ref.shape[0]
    key_live = lax.broadcasted_iota(jnp.int32, (1, span), 1) < own_live
    for h in range(acc_ref.shape[1] // HD):
        c = head_cols(h)
        masked = scaled_scores(q_ref[:, c], k_ref[:, c], key_live)
        top = jnp.max(masked, axis=1, keepdims=True)
        weights = jnp.exp(masked - top).astype(jnp.bfloat16)
        v = v_ref[:, c]
        v_ext = jnp.concatenate([v, jnp.ones_like(v)], axis=1)
        both = jnp.dot(weights, v_ext, preferred_element_type=jnp.float32)
        acc_ref[:, c] = both[:, :HD]
        top_ref[:, h : h + 1] = top
        tot_ref[:, h : h + 1] = both[:, HD : HD + 1]


def mscore_kernel(counts, q_ref, mk_ref, w_ref, top_ref, tot_ref):
    mot_start = (MOT_CAP - counts[1]) * FT
    tail = mk_ref.shape[0]
    slot_live = lax.broadcasted_iota(jnp.int32, (1, tail), 1) >= mot_start
    ones = jnp.ones((tail, HD), jnp.bfloat16)
    for h in range(q_ref.shape[1] // HD):
        c = head_cols(h)
        masked = scaled_scores(q_ref[:, c], mk_ref[:, c], slot_live)
        top = jnp.max(masked, axis=1, keepdims=True)
        weights = jnp.exp(masked - top).astype(jnp.bfloat16)
        w_ref[:, h * tail : (h + 1) * tail] = weights
        total = jnp.dot(weights, ones, preferred_element_type=jnp.float32)
        top_ref[:, h : h + 1] = top
        tot_ref[:, h : h + 1] = total[:, 0:1]


def merge_kernel(
    counts, w_ref, mv_ref, acc_ref, top_ref, tot_ref, mtop_ref, mtot_ref, o_ref
):
    own_live = counts[0] * FT
    tail = mv_ref.shape[0]
    rows = pl.program_id(0) * TQ + lax.broadcasted_iota(jnp.int32, (TQ, 1), 0)
    row_live = rows < own_live
    for h in range(o_ref.shape[1] // HD):
        c = head_cols(h)
        acc_mot = jnp.dot(
            w_ref[:, h * tail : (h + 1) * tail],
            mv_ref[:, c],
            preferred_element_type=jnp.float32,
        )
        top_own = top_ref[:, h : h + 1]
        top_mot = mtop_ref[:, h : h + 1]
        peak = jnp.maximum(top_own, top_mot)
        factor_own = jnp.exp(top_own - peak)
        factor_mot = jnp.exp(top_mot - peak)
        scale = 1.0 / (
            tot_ref[:, h : h + 1] * factor_own + mtot_ref[:, h : h + 1] * factor_mot
        )
        mixed = (acc_ref[:, c] * factor_own + acc_mot * factor_mot) * scale
        o_ref[:, c] = jnp.where(row_live, mixed, 0.0).astype(o_ref.dtype)


def rows_of(width):
    return pl.BlockSpec((TQ, width), lambda i, c: (i, 0))


def whole(rows, width):
    return pl.BlockSpec((rows, width), lambda i, c: (0, 0))


def call(kernel, counts, operands, in_specs, outs, cost):
    span = operands[0].shape[0]
    shapes = [jax.ShapeDtypeStruct((span, w), t) for w, t in outs]
    return pl.pallas_call(
        kernel,
        out_shape=tuple(shapes),
        grid_spec=pltpu.PrefetchScalarGridSpec(
            num_scalar_prefetch=1,
            grid=(span // TQ,),
            in_specs=in_specs,
            out_specs=[rows_of(w) for w, _ in outs],
        ),
        compiler_params=pltpu.CompilerParams(dimension_semantics=("arbitrary",)),
        cost_estimate=cost,
    )(counts, *operands)


def relay_plan(mesh):
    where = [mesh.devices[c, 0, 0].coords for c in range(mesh.devices.shape[0])]
    inner, first, second = [], [], []
    for c in range(1, len(where)):
        (xs, ys, zs), (xr, yr, zr) = where[c - 1], where[c]
        via = [j for j, (x, y, z) in enumerate(where) if y == ys and z == zr]
        if ys == yr or not via:
            inner.append((c - 1, c))
        else:
            first.append((c - 1, via[0]))
            second.append((via[0], c))
    return inner, first, second


def body(plan, queries, keys, values, frames, motion):
    stretch_index = lax.axis_index("stretch")
    tail = MOT_CAP * FT
    count_own = frames[stretch_index]
    counts = jnp.stack([count_own, motion[stretch_index]]).astype(jnp.int32)
    tail_begin = (count_own - MOT_CAP) * FT
    groups = lax.axis_size("head")
    rows, width = keys.shape
    local = width // groups

    def by_target(x):
        return x.reshape(rows, groups, local).transpose(1, 0, 2)

    kv_send = jnp.stack([by_target(keys), by_target(values)], axis=1)
    kv_recv = lax.all_to_all(kv_send, "head", split_axis=0, concat_axis=0, tiled=True)
    kv_rows = kv_recv.transpose(1, 0, 2, 3).reshape(2, groups * rows, local)
    k_heads, v_heads = kv_rows[0], kv_rows[1]
    kv_tail = lax.dynamic_slice_in_dim(kv_rows, tail_begin, tail, 1)
    inner, first, second = plan
    half = tail // 2
    direct = jnp.concatenate([kv_tail[0], kv_tail[1, :half]], axis=0)
    direct_prior = from_behind(direct, "stretch", 1)
    v_far = kv_tail[1, half:]
    if first:
        v_far = lax.ppermute(v_far, "stretch", inner) + lax.ppermute(
            lax.ppermute(v_far, "stretch", first), "stretch", second
        )
    else:
        v_far = from_behind(v_far, "stretch", 1)
    v_prior = jnp.concatenate([direct_prior[tail:], v_far], axis=0)
    q_heads = lax.all_to_all(queries, "head", split_axis=1, concat_axis=0, tiled=True)
    span, local = q_heads.shape
    heads = local // HD
    f32 = jnp.float32
    acc, top, tot = call(
        own_kernel,
        counts,
        (q_heads, k_heads, v_heads),
        [rows_of(local), whole(span, local), whole(span, local)],
        [(local, f32), (COLS, f32), (COLS, f32)],
        pl.CostEstimate(
            flops=heads * 2 * span * span * 3 * HD,
            transcendentals=heads * span * span,
            bytes_accessed=3 * span * local * 2 + span * local * 4,
        ),
    )
    w_mot, mtop, mtot = call(
        mscore_kernel,
        counts,
        (q_heads, direct_prior),
        [rows_of(local), whole(tail, local)],
        [(heads * tail, jnp.bfloat16), (COLS, f32), (COLS, f32)],
        pl.CostEstimate(
            flops=heads * 2 * span * tail * 2 * HD,
            transcendentals=heads * span * tail,
            bytes_accessed=span * local * 2 + tail * local * 2 + span * heads * tail * 2,
        ),
    )
    (mixed,) = call(
        merge_kernel,
        counts,
        (w_mot, v_prior, acc, top, tot, mtop, mtot),
        [
            rows_of(heads * tail),
            whole(tail, local),
            rows_of(local),
            rows_of(COLS),
            rows_of(COLS),
            rows_of(COLS),
            rows_of(COLS),
        ],
        [(local, jnp.bfloat16)],
        pl.CostEstimate(
            flops=heads * 2 * span * tail * HD,
            transcendentals=2 * heads * span,
            bytes_accessed=span * heads * tail * 2 + span * local * 6 + tail * local * 2,
        ),
    )
    return lax.all_to_all(mixed, "head", split_axis=0, concat_axis=1, tiled=True)


def solution(mesh):
    placed = (
        P(("cfg", "stretch", "head"), None),
        P(("cfg", "stretch", "head"), None),
        P(("cfg", "stretch", "head"), None),
        P(),
        P(),
    )
    return jax.shard_map(
        functools.partial(body, relay_plan(mesh)),
        mesh=mesh,
        in_specs=placed,
        out_specs=P(("cfg", "stretch", "head"), None),
        check_vma=False,
    )
```

```python
import functools
import math

import jax
import jax.numpy as jnp
from jax import lax
from jax.experimental import pallas as pl
from jax.experimental.pallas import tpu as pltpu
from jax.sharding import PartitionSpec as P

HD = 128
FT = 128
MOT_CAP = 4

NEG = -1e30
TQ = 448
COLS = 8


def from_behind(shard, axis, by):
    size = lax.axis_size(axis)
    pairs = [(i, i + by) for i in range(size) if 0 <= i + by < size]
    return lax.ppermute(shard, axis, pairs)


def scaled_scores(q, k, live):
    scores = lax.dot_general(
        q, k, (((1,), (1,)), ((), ())), preferred_element_type=jnp.float32
    )
    scores = scores * (1.0 / math.sqrt(HD))
    return jnp.where(live, scores, NEG)


def head_cols(h):
    return slice(h * HD, (h + 1) * HD)


def own_kernel(counts, q_ref, k_ref, v_ref, acc_ref, top_ref, tot_ref):
    own_live = counts[0] * FT
    span = k_ref.shape[0]
    key_live = lax.broadcasted_iota(jnp.int32, (1, span), 1) < own_live
    for h in range(acc_ref.shape[1] // HD):
        c = head_cols(h)
        masked = scaled_scores(q_ref[:, c], k_ref[:, c], key_live)
        top = jnp.max(masked, axis=1, keepdims=True)
        weights = jnp.exp(masked - top).astype(jnp.bfloat16)
        v = v_ref[:, c]
        v_ext = jnp.concatenate([v, jnp.ones_like(v)], axis=1)
        both = jnp.dot(weights, v_ext, preferred_element_type=jnp.float32)
        acc_ref[:, c] = both[:, :HD]
        top_ref[:, h : h + 1] = top
        tot_ref[:, h : h + 1] = both[:, HD : HD + 1]


def mscore_kernel(counts, q_ref, mk_ref, w_ref, top_ref, tot_ref):
    mot_start = (MOT_CAP - counts[1]) * FT
    tail = mk_ref.shape[0]
    slot_live = lax.broadcasted_iota(jnp.int32, (1, tail), 1) >= mot_start
    ones = jnp.ones((tail, HD), jnp.bfloat16)
    for h in range(q_ref.shape[1] // HD):
        c = head_cols(h)
        masked = scaled_scores(q_ref[:, c], mk_ref[:, c], slot_live)
        top = jnp.max(masked, axis=1, keepdims=True)
        weights = jnp.exp(masked - top).astype(jnp.bfloat16)
        w_ref[:, h * tail : (h + 1) * tail] = weights
        total = jnp.dot(weights, ones, preferred_element_type=jnp.float32)
        top_ref[:, h : h + 1] = top
        tot_ref[:, h : h + 1] = total[:, 0:1]


def merge_kernel(
    counts, w_ref, mv_ref, acc_ref, top_ref, tot_ref, mtop_ref, mtot_ref, o_ref
):
    own_live = counts[0] * FT
    tail = mv_ref.shape[0]
    rows = pl.program_id(0) * TQ + lax.broadcasted_iota(jnp.int32, (TQ, 1), 0)
    row_live = rows < own_live
    for h in range(o_ref.shape[1] // HD):
        c = head_cols(h)
        acc_mot = jnp.dot(
            w_ref[:, h * tail : (h + 1) * tail],
            mv_ref[:, c],
            preferred_element_type=jnp.float32,
        )
        top_own = top_ref[:, h : h + 1]
        top_mot = mtop_ref[:, h : h + 1]
        peak = jnp.maximum(top_own, top_mot)
        factor_own = jnp.exp(top_own - peak)
        factor_mot = jnp.exp(top_mot - peak)
        scale = 1.0 / (
            tot_ref[:, h : h + 1] * factor_own + mtot_ref[:, h : h + 1] * factor_mot
        )
        mixed = (acc_ref[:, c] * factor_own + acc_mot * factor_mot) * scale
        o_ref[:, c] = jnp.where(row_live, mixed, 0.0).astype(o_ref.dtype)


def rows_of(width):
    return pl.BlockSpec((TQ, width), lambda i, c: (i, 0))


def whole(rows, width):
    return pl.BlockSpec((rows, width), lambda i, c: (0, 0))


def call(kernel, counts, operands, in_specs, outs, cost):
    span = operands[0].shape[0]
    shapes = [jax.ShapeDtypeStruct((span, w), t) for w, t in outs]
    return pl.pallas_call(
        kernel,
        out_shape=tuple(shapes),
        grid_spec=pltpu.PrefetchScalarGridSpec(
            num_scalar_prefetch=1,
            grid=(span // TQ,),
            in_specs=in_specs,
            out_specs=[rows_of(w) for w, _ in outs],
        ),
        compiler_params=pltpu.CompilerParams(dimension_semantics=("arbitrary",)),
        cost_estimate=cost,
    )(counts, *operands)


def relay_plan(mesh):
    where = [mesh.devices[c, 0, 0].coords for c in range(mesh.devices.shape[0])]
    inner, first, second = [], [], []
    for c in range(1, len(where)):
        (xs, ys, zs), (xr, yr, zr) = where[c - 1], where[c]
        via = [j for j, (x, y, z) in enumerate(where) if y == ys and z == zr]
        if ys == yr or not via:
            inner.append((c - 1, c))
        else:
            first.append((c - 1, via[0]))
            second.append((via[0], c))
    return inner, first, second


def body(plan, queries, keys, values, frames, motion):
    stretch_index = lax.axis_index("stretch")
    tail = MOT_CAP * FT
    count_own = frames[stretch_index]
    counts = jnp.stack([count_own, motion[stretch_index]]).astype(jnp.int32)
    tail_begin = (count_own - MOT_CAP) * FT
    groups = lax.axis_size("head")
    rows, width = keys.shape
    local = width // groups

    def by_target(x):
        return x.reshape(rows, groups, local).transpose(1, 0, 2)

    kv_send = jnp.stack([by_target(keys), by_target(values)], axis=1)
    kv_recv = lax.all_to_all(kv_send, "head", split_axis=0, concat_axis=0, tiled=True)
    kv_rows = kv_recv.transpose(1, 0, 2, 3).reshape(2, groups * rows, local)
    k_heads, v_heads = kv_rows[0], kv_rows[1]
    k_tail = lax.dynamic_slice_in_dim(k_heads, tail_begin, tail, 0)
    v_tail = lax.dynamic_slice_in_dim(v_heads, tail_begin, tail, 0)
    k_prior = from_behind(k_tail, "stretch", 1)
    inner, first, second = plan
    half = tail // 2
    v_near = v_tail[:half]
    v_far = v_tail[half:]
    if first:
        v_far = lax.ppermute(v_far, "stretch", inner) + lax.ppermute(
            lax.ppermute(v_far, "stretch", first), "stretch", second
        )
    else:
        v_far = from_behind(v_far, "stretch", 1)
    q_heads = lax.all_to_all(queries, "head", split_axis=1, concat_axis=0, tiled=True)
    span, local = q_heads.shape
    heads = local // HD
    f32 = jnp.float32
    acc, top, tot = call(
        own_kernel,
        counts,
        (q_heads, k_heads, v_heads),
        [rows_of(local), whole(span, local), whole(span, local)],
        [(local, f32), (COLS, f32), (COLS, f32)],
        pl.CostEstimate(
            flops=heads * 2 * span * span * 3 * HD,
            transcendentals=heads * span * span,
            bytes_accessed=3 * span * local * 2 + span * local * 4,
        ),
    )
    v_near, k_prior, acc = lax.optimization_barrier((v_near, k_prior, acc))
    v_near = from_behind(v_near, "stretch", 1)
    v_prior = jnp.concatenate([v_near, v_far], axis=0)
    w_mot, mtop, mtot = call(
        mscore_kernel,
        counts,
        (q_heads, k_prior),
        [rows_of(local), whole(tail, local)],
        [(heads * tail, jnp.bfloat16), (COLS, f32), (COLS, f32)],
        pl.CostEstimate(
            flops=heads * 2 * span * tail * 2 * HD,
            transcendentals=heads * span * tail,
            bytes_accessed=span * local * 2 + tail * local * 2 + span * heads * tail * 2,
        ),
    )
    (mixed,) = call(
        merge_kernel,
        counts,
        (w_mot, v_prior, acc, top, tot, mtop, mtot),
        [
            rows_of(heads * tail),
            whole(tail, local),
            rows_of(local),
            rows_of(COLS),
            rows_of(COLS),
            rows_of(COLS),
            rows_of(COLS),
        ],
        [(local, jnp.bfloat16)],
        pl.CostEstimate(
            flops=heads * 2 * span * tail * HD,
            transcendentals=2 * heads * span,
            bytes_accessed=span * heads * tail * 2 + span * local * 6 + tail * local * 2,
        ),
    )
    return lax.all_to_all(mixed, "head", split_axis=0, concat_axis=1, tiled=True)


def solution(mesh):
    placed = (
        P(("cfg", "stretch", "head"), None),
        P(("cfg", "stretch", "head"), None),
        P(("cfg", "stretch", "head"), None),
        P(),
        P(),
    )
    return jax.shard_map(
        functools.partial(body, relay_plan(mesh)),
        mesh=mesh,
        in_specs=placed,
        out_specs=P(("cfg", "stretch", "head"), None),
        check_vma=False,
    )
```

```python
import functools
import math

import jax
import jax.numpy as jnp
from jax import lax
from jax.experimental import pallas as pl
from jax.experimental.pallas import tpu as pltpu
from jax.sharding import PartitionSpec as P

HD = 128
FT = 128
MOT_CAP = 4

NEG = -1e30
TQ = 448
COLS = 8


def from_behind(shard, axis, by):
    size = lax.axis_size(axis)
    pairs = [(i, i + by) for i in range(size) if 0 <= i + by < size]
    return lax.ppermute(shard, axis, pairs)


def scaled_scores(q, k, live):
    scores = lax.dot_general(
        q, k, (((1,), (1,)), ((), ())), preferred_element_type=jnp.float32
    )
    scores = scores * (1.0 / math.sqrt(HD))
    return jnp.where(live, scores, NEG)


def head_cols(h):
    return slice(h * HD, (h + 1) * HD)


def own_kernel(counts, q_ref, k_ref, v_ref, acc_ref, top_ref, tot_ref):
    own_live = counts[0] * FT
    span = k_ref.shape[0]
    key_live = lax.broadcasted_iota(jnp.int32, (1, span), 1) < own_live
    for h in range(acc_ref.shape[1] // HD):
        c = head_cols(h)
        masked = scaled_scores(q_ref[:, c], k_ref[:, c], key_live)
        top = jnp.max(masked, axis=1, keepdims=True)
        weights = jnp.exp(masked - top).astype(jnp.bfloat16)
        v = v_ref[:, c]
        v_ext = jnp.concatenate([v, jnp.ones_like(v)], axis=1)
        both = jnp.dot(weights, v_ext, preferred_element_type=jnp.float32)
        acc_ref[:, c] = both[:, :HD]
        top_ref[:, h : h + 1] = top
        tot_ref[:, h : h + 1] = both[:, HD : HD + 1]


def mscore_kernel(counts, q_ref, mk_ref, w_ref, top_ref, tot_ref):
    mot_start = (MOT_CAP - counts[1]) * FT
    tail = mk_ref.shape[0]
    slot_live = lax.broadcasted_iota(jnp.int32, (1, tail), 1) >= mot_start
    ones = jnp.ones((tail, HD), jnp.bfloat16)
    for h in range(q_ref.shape[1] // HD):
        c = head_cols(h)
        masked = scaled_scores(q_ref[:, c], mk_ref[:, c], slot_live)
        top = jnp.max(masked, axis=1, keepdims=True)
        weights = jnp.exp(masked - top).astype(jnp.bfloat16)
        w_ref[:, h * tail : (h + 1) * tail] = weights
        total = jnp.dot(weights, ones, preferred_element_type=jnp.float32)
        top_ref[:, h : h + 1] = top
        tot_ref[:, h : h + 1] = total[:, 0:1]


def merge_kernel(
    counts, w_ref, mv_ref, acc_ref, top_ref, tot_ref, mtop_ref, mtot_ref, o_ref
):
    own_live = counts[0] * FT
    tail = mv_ref.shape[0]
    rows = pl.program_id(0) * TQ + lax.broadcasted_iota(jnp.int32, (TQ, 1), 0)
    row_live = rows < own_live
    for h in range(o_ref.shape[1] // HD):
        c = head_cols(h)
        acc_mot = jnp.dot(
            w_ref[:, h * tail : (h + 1) * tail],
            mv_ref[:, c],
            preferred_element_type=jnp.float32,
        )
        top_own = top_ref[:, h : h + 1]
        top_mot = mtop_ref[:, h : h + 1]
        peak = jnp.maximum(top_own, top_mot)
        factor_own = jnp.exp(top_own - peak)
        factor_mot = jnp.exp(top_mot - peak)
        scale = 1.0 / (
            tot_ref[:, h : h + 1] * factor_own + mtot_ref[:, h : h + 1] * factor_mot
        )
        mixed = (acc_ref[:, c] * factor_own + acc_mot * factor_mot) * scale
        o_ref[:, c] = jnp.where(row_live, mixed, 0.0).astype(o_ref.dtype)


def rows_of(width):
    return pl.BlockSpec((TQ, width), lambda i, c: (i, 0))


def whole(rows, width):
    return pl.BlockSpec((rows, width), lambda i, c: (0, 0))


def call(kernel, counts, operands, in_specs, outs, cost):
    span = operands[0].shape[0]
    shapes = [jax.ShapeDtypeStruct((span, w), t) for w, t in outs]
    return pl.pallas_call(
        kernel,
        out_shape=tuple(shapes),
        grid_spec=pltpu.PrefetchScalarGridSpec(
            num_scalar_prefetch=1,
            grid=(span // TQ,),
            in_specs=in_specs,
            out_specs=[rows_of(w) for w, _ in outs],
        ),
        compiler_params=pltpu.CompilerParams(dimension_semantics=("arbitrary",)),
        cost_estimate=cost,
    )(counts, *operands)


def relay_plan(mesh):
    where = [mesh.devices[c, 0, 0].coords for c in range(mesh.devices.shape[0])]
    inner, first, second = [], [], []
    for c in range(1, len(where)):
        (xs, ys, zs), (xr, yr, zr) = where[c - 1], where[c]
        via = [j for j, (x, y, z) in enumerate(where) if y == ys and z == zr]
        if ys == yr or not via:
            inner.append((c - 1, c))
        else:
            first.append((c - 1, via[0]))
            second.append((via[0], c))
    return inner, first, second


def body(plan, queries, keys, values, frames, motion):
    stretch_index = lax.axis_index("stretch")
    tail = MOT_CAP * FT
    count_own = frames[stretch_index]
    counts = jnp.stack([count_own, motion[stretch_index]]).astype(jnp.int32)
    tail_begin = (count_own - MOT_CAP) * FT
    groups = lax.axis_size("head")
    rows, width = keys.shape
    local = width // groups

    def by_target(x):
        return x.reshape(rows, groups, local).transpose(1, 0, 2)

    kv_send = jnp.stack([by_target(keys), by_target(values)], axis=1)
    kv_recv = lax.all_to_all(kv_send, "head", split_axis=0, concat_axis=0, tiled=True)
    kv_rows = kv_recv.transpose(1, 0, 2, 3).reshape(2, groups * rows, local)
    k_heads, v_heads = kv_rows[0], kv_rows[1]
    k_tail = lax.dynamic_slice_in_dim(k_heads, tail_begin, tail, 0)
    v_tail = lax.dynamic_slice_in_dim(v_heads, tail_begin, tail, 0)
    k_prior = from_behind(k_tail, "stretch", 1)
    inner, first, second = plan
    half = tail // 4
    v_near = from_behind(v_tail[:half], "stretch", 1)
    v_far = v_tail[half:]
    if first:
        v_far = lax.ppermute(v_far, "stretch", inner) + lax.ppermute(
            lax.ppermute(v_far, "stretch", first), "stretch", second
        )
    else:
        v_far = from_behind(v_far, "stretch", 1)
    v_prior = jnp.concatenate([v_near, v_far], axis=0)
    q_heads = lax.all_to_all(queries, "head", split_axis=1, concat_axis=0, tiled=True)
    span, local = q_heads.shape
    heads = local // HD
    f32 = jnp.float32
    acc, top, tot = call(
        own_kernel,
        counts,
        (q_heads, k_heads, v_heads),
        [rows_of(local), whole(span, local), whole(span, local)],
        [(local, f32), (COLS, f32), (COLS, f32)],
        pl.CostEstimate(
            flops=heads * 2 * span * span * 3 * HD,
            transcendentals=heads * span * span,
            bytes_accessed=3 * span * local * 2 + span * local * 4,
        ),
    )
    w_mot, mtop, mtot = call(
        mscore_kernel,
        counts,
        (q_heads, k_prior),
        [rows_of(local), whole(tail, local)],
        [(heads * tail, jnp.bfloat16), (COLS, f32), (COLS, f32)],
        pl.CostEstimate(
            flops=heads * 2 * span * tail * 2 * HD,
            transcendentals=heads * span * tail,
            bytes_accessed=span * local * 2 + tail * local * 2 + span * heads * tail * 2,
        ),
    )
    (mixed,) = call(
        merge_kernel,
        counts,
        (w_mot, v_prior, acc, top, tot, mtop, mtot),
        [
            rows_of(heads * tail),
            whole(tail, local),
            rows_of(local),
            rows_of(COLS),
            rows_of(COLS),
            rows_of(COLS),
            rows_of(COLS),
        ],
        [(local, jnp.bfloat16)],
        pl.CostEstimate(
            flops=heads * 2 * span * tail * HD,
            transcendentals=2 * heads * span,
            bytes_accessed=span * heads * tail * 2 + span * local * 6 + tail * local * 2,
        ),
    )
    return lax.all_to_all(mixed, "head", split_axis=0, concat_axis=1, tiled=True)


def solution(mesh):
    placed = (
        P(("cfg", "stretch", "head"), None),
        P(("cfg", "stretch", "head"), None),
        P(("cfg", "stretch", "head"), None),
        P(),
        P(),
    )
    return jax.shard_map(
        functools.partial(body, relay_plan(mesh)),
        mesh=mesh,
        in_specs=placed,
        out_specs=P(("cfg", "stretch", "head"), None),
        check_vma=False,
    )
```

```python
import functools
import math

import jax
import jax.numpy as jnp
from jax import lax
from jax.experimental import pallas as pl
from jax.experimental.pallas import tpu as pltpu
from jax.sharding import PartitionSpec as P

HD = 128
FT = 128
MOT_CAP = 4

NEG = -1e30
TQ = 448
COLS = 8


def from_behind(shard, axis, by):
    size = lax.axis_size(axis)
    pairs = [(i, i + by) for i in range(size) if 0 <= i + by < size]
    return lax.ppermute(shard, axis, pairs)


def scaled_scores(q, k, live):
    scores = lax.dot_general(
        q, k, (((1,), (1,)), ((), ())), preferred_element_type=jnp.float32
    )
    scores = scores * (1.0 / math.sqrt(HD))
    return jnp.where(live, scores, NEG)


def head_cols(h):
    return slice(h * HD, (h + 1) * HD)


def own_kernel(counts, q_ref, k_ref, v_ref, acc_ref, top_ref, tot_ref):
    own_live = counts[0] * FT
    span = k_ref.shape[0]
    key_live = lax.broadcasted_iota(jnp.int32, (1, span), 1) < own_live
    for h in range(acc_ref.shape[1] // HD):
        c = head_cols(h)
        masked = scaled_scores(q_ref[:, c], k_ref[:, c], key_live)
        top = jnp.max(masked, axis=1, keepdims=True)
        weights = jnp.exp(masked - top).astype(jnp.bfloat16)
        v = v_ref[:, c]
        v_ext = jnp.concatenate([v, jnp.ones_like(v)], axis=1)
        both = jnp.dot(weights, v_ext, preferred_element_type=jnp.float32)
        acc_ref[:, c] = both[:, :HD]
        top_ref[:, h : h + 1] = top
        tot_ref[:, h : h + 1] = both[:, HD : HD + 1]


def mscore_kernel(counts, q_ref, mk_ref, w_ref, top_ref, tot_ref):
    mot_start = (MOT_CAP - counts[1]) * FT
    tail = mk_ref.shape[0]
    slot_live = lax.broadcasted_iota(jnp.int32, (1, tail), 1) >= mot_start
    ones = jnp.ones((tail, HD), jnp.bfloat16)
    for h in range(q_ref.shape[1] // HD):
        c = head_cols(h)
        masked = scaled_scores(q_ref[:, c], mk_ref[:, c], slot_live)
        top = jnp.max(masked, axis=1, keepdims=True)
        weights = jnp.exp(masked - top).astype(jnp.bfloat16)
        w_ref[:, h * tail : (h + 1) * tail] = weights
        total = jnp.dot(weights, ones, preferred_element_type=jnp.float32)
        top_ref[:, h : h + 1] = top
        tot_ref[:, h : h + 1] = total[:, 0:1]


def merge_kernel(
    counts, w_ref, mv_ref, acc_ref, top_ref, tot_ref, mtop_ref, mtot_ref, o_ref
):
    own_live = counts[0] * FT
    tail = mv_ref.shape[0]
    rows = pl.program_id(0) * TQ + lax.broadcasted_iota(jnp.int32, (TQ, 1), 0)
    row_live = rows < own_live
    for h in range(o_ref.shape[1] // HD):
        c = head_cols(h)
        acc_mot = jnp.dot(
            w_ref[:, h * tail : (h + 1) * tail],
            mv_ref[:, c],
            preferred_element_type=jnp.float32,
        )
        top_own = top_ref[:, h : h + 1]
        top_mot = mtop_ref[:, h : h + 1]
        peak = jnp.maximum(top_own, top_mot)
        factor_own = jnp.exp(top_own - peak)
        factor_mot = jnp.exp(top_mot - peak)
        scale = 1.0 / (
            tot_ref[:, h : h + 1] * factor_own + mtot_ref[:, h : h + 1] * factor_mot
        )
        mixed = (acc_ref[:, c] * factor_own + acc_mot * factor_mot) * scale
        o_ref[:, c] = jnp.where(row_live, mixed, 0.0).astype(o_ref.dtype)


def rows_of(width):
    return pl.BlockSpec((TQ, width), lambda i, c: (i, 0))


def whole(rows, width):
    return pl.BlockSpec((rows, width), lambda i, c: (0, 0))


def call(kernel, counts, operands, in_specs, outs, cost):
    span = operands[0].shape[0]
    shapes = [jax.ShapeDtypeStruct((span, w), t) for w, t in outs]
    return pl.pallas_call(
        kernel,
        out_shape=tuple(shapes),
        grid_spec=pltpu.PrefetchScalarGridSpec(
            num_scalar_prefetch=1,
            grid=(span // TQ,),
            in_specs=in_specs,
            out_specs=[rows_of(w) for w, _ in outs],
        ),
        compiler_params=pltpu.CompilerParams(dimension_semantics=("arbitrary",)),
        cost_estimate=cost,
    )(counts, *operands)


def relay_plan(mesh):
    where = [mesh.devices[c, 0, 0].coords for c in range(mesh.devices.shape[0])]
    inner, first, second = [], [], []
    for c in range(1, len(where)):
        (xs, ys, zs), (xr, yr, zr) = where[c - 1], where[c]
        via = [j for j, (x, y, z) in enumerate(where) if y == ys and z == zr]
        if ys == yr or not via:
            inner.append((c - 1, c))
        else:
            first.append((c - 1, via[0]))
            second.append((via[0], c))
    return inner, first, second


def body(plan, queries, keys, values, frames, motion):
    stretch_index = lax.axis_index("stretch")
    tail = MOT_CAP * FT
    count_own = frames[stretch_index]
    counts = jnp.stack([count_own, motion[stretch_index]]).astype(jnp.int32)
    tail_begin = (count_own - MOT_CAP) * FT
    groups = lax.axis_size("head")
    rows, width = keys.shape
    local = width // groups

    def by_target(x):
        return x.reshape(rows, groups, local).transpose(1, 0, 2)

    kv_send = jnp.stack([by_target(keys), by_target(values)], axis=1)
    kv_recv = lax.all_to_all(kv_send, "head", split_axis=0, concat_axis=0, tiled=True)
    kv_rows = kv_recv.transpose(1, 0, 2, 3).reshape(2, groups * rows, local)
    k_heads, v_heads = kv_rows[0], kv_rows[1]
    k_tail = lax.dynamic_slice_in_dim(k_heads, tail_begin, tail, 0)
    v_tail = lax.dynamic_slice_in_dim(v_heads, tail_begin, tail, 0)
    k_prior = from_behind(k_tail, "stretch", 1)
    inner, first, second = plan
    half = tail // 8
    v_near = from_behind(v_tail[:half], "stretch", 1)
    v_far = v_tail[half:]
    if first:
        v_far = lax.ppermute(v_far, "stretch", inner) + lax.ppermute(
            lax.ppermute(v_far, "stretch", first), "stretch", second
        )
    else:
        v_far = from_behind(v_far, "stretch", 1)
    v_prior = jnp.concatenate([v_near, v_far], axis=0)
    q_heads = lax.all_to_all(queries, "head", split_axis=1, concat_axis=0, tiled=True)
    span, local = q_heads.shape
    heads = local // HD
    f32 = jnp.float32
    acc, top, tot = call(
        own_kernel,
        counts,
        (q_heads, k_heads, v_heads),
        [rows_of(local), whole(span, local), whole(span, local)],
        [(local, f32), (COLS, f32), (COLS, f32)],
        pl.CostEstimate(
            flops=heads * 2 * span * span * 3 * HD,
            transcendentals=heads * span * span,
            bytes_accessed=3 * span * local * 2 + span * local * 4,
        ),
    )
    w_mot, mtop, mtot = call(
        mscore_kernel,
        counts,
        (q_heads, k_prior),
        [rows_of(local), whole(tail, local)],
        [(heads * tail, jnp.bfloat16), (COLS, f32), (COLS, f32)],
        pl.CostEstimate(
            flops=heads * 2 * span * tail * 2 * HD,
            transcendentals=heads * span * tail,
            bytes_accessed=span * local * 2 + tail * local * 2 + span * heads * tail * 2,
        ),
    )
    (mixed,) = call(
        merge_kernel,
        counts,
        (w_mot, v_prior, acc, top, tot, mtop, mtot),
        [
            rows_of(heads * tail),
            whole(tail, local),
            rows_of(local),
            rows_of(COLS),
            rows_of(COLS),
            rows_of(COLS),
            rows_of(COLS),
        ],
        [(local, jnp.bfloat16)],
        pl.CostEstimate(
            flops=heads * 2 * span * tail * HD,
            transcendentals=2 * heads * span,
            bytes_accessed=span * heads * tail * 2 + span * local * 6 + tail * local * 2,
        ),
    )
    return lax.all_to_all(mixed, "head", split_axis=0, concat_axis=1, tiled=True)


def solution(mesh):
    placed = (
        P(("cfg", "stretch", "head"), None),
        P(("cfg", "stretch", "head"), None),
        P(("cfg", "stretch", "head"), None),
        P(),
        P(),
    )
    return jax.shard_map(
        functools.partial(body, relay_plan(mesh)),
        mesh=mesh,
        in_specs=placed,
        out_specs=P(("cfg", "stretch", "head"), None),
        check_vma=False,
    )
```

```python
import functools
import math

import jax
import jax.numpy as jnp
from jax import lax
from jax.experimental import pallas as pl
from jax.experimental.pallas import tpu as pltpu
from jax.sharding import PartitionSpec as P

HD = 128
FT = 128
MOT_CAP = 4

NEG = -1e30
TQ = 448
COLS = 8


def from_behind(shard, axis, by):
    size = lax.axis_size(axis)
    pairs = [(i, i + by) for i in range(size) if 0 <= i + by < size]
    return lax.ppermute(shard, axis, pairs)


def scaled_scores(q, k, live):
    scores = lax.dot_general(
        q, k, (((1,), (1,)), ((), ())), preferred_element_type=jnp.float32
    )
    scores = scores * (1.0 / math.sqrt(HD))
    return jnp.where(live, scores, NEG)


def head_cols(h):
    return slice(h * HD, (h + 1) * HD)


def own_kernel(counts, q_ref, k_ref, v_ref, acc_ref, top_ref, tot_ref):
    own_live = counts[0] * FT
    span = k_ref.shape[0]
    key_live = lax.broadcasted_iota(jnp.int32, (1, span), 1) < own_live
    for h in range(acc_ref.shape[1] // HD):
        c = head_cols(h)
        masked = scaled_scores(q_ref[:, c], k_ref[:, c], key_live)
        top = jnp.max(masked, axis=1, keepdims=True)
        weights = jnp.exp(masked - top).astype(jnp.bfloat16)
        v = v_ref[:, c]
        v_ext = jnp.concatenate([v, jnp.ones_like(v)], axis=1)
        both = jnp.dot(weights, v_ext, preferred_element_type=jnp.float32)
        acc_ref[:, c] = both[:, :HD]
        top_ref[:, h : h + 1] = top
        tot_ref[:, h : h + 1] = both[:, HD : HD + 1]


def mscore_kernel(counts, q_ref, mk_ref, w_ref, top_ref, tot_ref):
    mot_start = (MOT_CAP - counts[1]) * FT
    tail = mk_ref.shape[0]
    slot_live = lax.broadcasted_iota(jnp.int32, (1, tail), 1) >= mot_start
    ones = jnp.ones((tail, HD), jnp.bfloat16)
    for h in range(q_ref.shape[1] // HD):
        c = head_cols(h)
        masked = scaled_scores(q_ref[:, c], mk_ref[:, c], slot_live)
        top = jnp.max(masked, axis=1, keepdims=True)
        weights = jnp.exp(masked - top).astype(jnp.bfloat16)
        w_ref[:, h * tail : (h + 1) * tail] = weights
        total = jnp.dot(weights, ones, preferred_element_type=jnp.float32)
        top_ref[:, h : h + 1] = top
        tot_ref[:, h : h + 1] = total[:, 0:1]


def merge_kernel(
    counts, w_ref, mv_ref, acc_ref, top_ref, tot_ref, mtop_ref, mtot_ref, o_ref
):
    own_live = counts[0] * FT
    tail = mv_ref.shape[0]
    rows = pl.program_id(0) * TQ + lax.broadcasted_iota(jnp.int32, (TQ, 1), 0)
    row_live = rows < own_live
    for h in range(o_ref.shape[1] // HD):
        c = head_cols(h)
        acc_mot = jnp.dot(
            w_ref[:, h * tail : (h + 1) * tail],
            mv_ref[:, c],
            preferred_element_type=jnp.float32,
        )
        top_own = top_ref[:, h : h + 1]
        top_mot = mtop_ref[:, h : h + 1]
        peak = jnp.maximum(top_own, top_mot)
        factor_own = jnp.exp(top_own - peak)
        factor_mot = jnp.exp(top_mot - peak)
        scale = 1.0 / (
            tot_ref[:, h : h + 1] * factor_own + mtot_ref[:, h : h + 1] * factor_mot
        )
        mixed = (acc_ref[:, c] * factor_own + acc_mot * factor_mot) * scale
        o_ref[:, c] = jnp.where(row_live, mixed, 0.0).astype(o_ref.dtype)


def rows_of(width):
    return pl.BlockSpec((TQ, width), lambda i, c: (i, 0))


def whole(rows, width):
    return pl.BlockSpec((rows, width), lambda i, c: (0, 0))


def call(kernel, counts, operands, in_specs, outs, cost):
    span = operands[0].shape[0]
    shapes = [jax.ShapeDtypeStruct((span, w), t) for w, t in outs]
    return pl.pallas_call(
        kernel,
        out_shape=tuple(shapes),
        grid_spec=pltpu.PrefetchScalarGridSpec(
            num_scalar_prefetch=1,
            grid=(span // TQ,),
            in_specs=in_specs,
            out_specs=[rows_of(w) for w, _ in outs],
        ),
        compiler_params=pltpu.CompilerParams(dimension_semantics=("arbitrary",)),
        cost_estimate=cost,
    )(counts, *operands)


def relay_plan(mesh):
    where = [mesh.devices[c, 0, 0].coords for c in range(mesh.devices.shape[0])]
    inner, first, second = [], [], []
    for c in range(1, len(where)):
        (xs, ys, zs), (xr, yr, zr) = where[c - 1], where[c]
        via = [j for j, (x, y, z) in enumerate(where) if y == ys and z == zr]
        if ys == yr or not via:
            inner.append((c - 1, c))
        else:
            first.append((c - 1, via[0]))
            second.append((via[0], c))
    return inner, first, second


def body(plan, queries, keys, values, frames, motion):
    stretch_index = lax.axis_index("stretch")
    tail = MOT_CAP * FT
    count_own = frames[stretch_index]
    counts = jnp.stack([count_own, motion[stretch_index]]).astype(jnp.int32)
    tail_begin = (count_own - MOT_CAP) * FT
    groups = lax.axis_size("head")
    rows, width = keys.shape
    local = width // groups

    def by_target(x):
        return x.reshape(rows, groups, local).transpose(1, 0, 2)

    kv_send = jnp.stack([by_target(keys), by_target(values)], axis=1)
    kv_recv = lax.all_to_all(kv_send, "head", split_axis=0, concat_axis=0, tiled=True)
    kv_rows = kv_recv.transpose(1, 0, 2, 3).reshape(2, groups * rows, local)
    k_heads, v_heads = kv_rows[0], kv_rows[1]
    k_tail = lax.dynamic_slice_in_dim(k_heads, tail_begin, tail, 0)
    v_tail = lax.dynamic_slice_in_dim(v_heads, tail_begin, tail, 0)
    k_prior = from_behind(k_tail, "stretch", 1)
    inner, first, second = plan
    half = 3 * tail // 8
    v_near = from_behind(v_tail[:half], "stretch", 1)
    v_far = v_tail[half:]
    if first:
        v_far = lax.ppermute(v_far, "stretch", inner) + lax.ppermute(
            lax.ppermute(v_far, "stretch", first), "stretch", second
        )
    else:
        v_far = from_behind(v_far, "stretch", 1)
    v_prior = jnp.concatenate([v_near, v_far], axis=0)
    q_heads = lax.all_to_all(queries, "head", split_axis=1, concat_axis=0, tiled=True)
    span, local = q_heads.shape
    heads = local // HD
    f32 = jnp.float32
    acc, top, tot = call(
        own_kernel,
        counts,
        (q_heads, k_heads, v_heads),
        [rows_of(local), whole(span, local), whole(span, local)],
        [(local, f32), (COLS, f32), (COLS, f32)],
        pl.CostEstimate(
            flops=heads * 2 * span * span * 3 * HD,
            transcendentals=heads * span * span,
            bytes_accessed=3 * span * local * 2 + span * local * 4,
        ),
    )
    w_mot, mtop, mtot = call(
        mscore_kernel,
        counts,
        (q_heads, k_prior),
        [rows_of(local), whole(tail, local)],
        [(heads * tail, jnp.bfloat16), (COLS, f32), (COLS, f32)],
        pl.CostEstimate(
            flops=heads * 2 * span * tail * 2 * HD,
            transcendentals=heads * span * tail,
            bytes_accessed=span * local * 2 + tail * local * 2 + span * heads * tail * 2,
        ),
    )
    (mixed,) = call(
        merge_kernel,
        counts,
        (w_mot, v_prior, acc, top, tot, mtop, mtot),
        [
            rows_of(heads * tail),
            whole(tail, local),
            rows_of(local),
            rows_of(COLS),
            rows_of(COLS),
            rows_of(COLS),
            rows_of(COLS),
        ],
        [(local, jnp.bfloat16)],
        pl.CostEstimate(
            flops=heads * 2 * span * tail * HD,
            transcendentals=2 * heads * span,
            bytes_accessed=span * heads * tail * 2 + span * local * 6 + tail * local * 2,
        ),
    )
    return lax.all_to_all(mixed, "head", split_axis=0, concat_axis=1, tiled=True)


def solution(mesh):
    placed = (
        P(("cfg", "stretch", "head"), None),
        P(("cfg", "stretch", "head"), None),
        P(("cfg", "stretch", "head"), None),
        P(),
        P(),
    )
    return jax.shard_map(
        functools.partial(body, relay_plan(mesh)),
        mesh=mesh,
        in_specs=placed,
        out_specs=P(("cfg", "stretch", "head"), None),
        check_vma=False,
    )
```

```python
import functools
import math

import jax
import jax.numpy as jnp
from jax import lax
from jax.experimental import pallas as pl
from jax.experimental.pallas import tpu as pltpu
from jax.sharding import PartitionSpec as P

HD = 128
FT = 128
MOT_CAP = 4

NEG = -1e30
TQ = 448
COLS = 8
PAIR = 2 * COLS


def from_behind(shard, axis, by):
    size = lax.axis_size(axis)
    pairs = [(i, i + by) for i in range(size) if 0 <= i + by < size]
    return lax.ppermute(shard, axis, pairs)


def scaled_scores(q, k, live):
    scores = lax.dot_general(
        q, k, (((1,), (1,)), ((), ())), preferred_element_type=jnp.float32
    )
    scores = scores * (1.0 / math.sqrt(HD))
    return jnp.where(live, scores, NEG)


def head_cols(h):
    return slice(h * HD, (h + 1) * HD)


def own_kernel(counts, q_ref, k_ref, v_ref, acc_ref, stat_ref):
    own_live = counts[0] * FT
    span = k_ref.shape[0]
    key_live = lax.broadcasted_iota(jnp.int32, (1, span), 1) < own_live
    for h in range(acc_ref.shape[1] // HD):
        c = head_cols(h)
        masked = scaled_scores(q_ref[:, c], k_ref[:, c], key_live)
        top = jnp.max(masked, axis=1, keepdims=True)
        weights = jnp.exp(masked - top).astype(jnp.bfloat16)
        v = v_ref[:, c]
        v_ext = jnp.concatenate([v, jnp.ones_like(v)], axis=1)
        both = jnp.dot(weights, v_ext, preferred_element_type=jnp.float32)
        acc_ref[:, c] = both[:, :HD]
        stat_ref[:, h : h + 1] = top
        stat_ref[:, COLS + h : COLS + h + 1] = both[:, HD : HD + 1]


def mscore_kernel(counts, q_ref, mk_ref, w_ref, stat_ref):
    mot_start = (MOT_CAP - counts[1]) * FT
    tail = mk_ref.shape[0]
    slot_live = lax.broadcasted_iota(jnp.int32, (1, tail), 1) >= mot_start
    ones = jnp.ones((tail, HD), jnp.bfloat16)
    for h in range(q_ref.shape[1] // HD):
        c = head_cols(h)
        masked = scaled_scores(q_ref[:, c], mk_ref[:, c], slot_live)
        top = jnp.max(masked, axis=1, keepdims=True)
        weights = jnp.exp(masked - top).astype(jnp.bfloat16)
        w_ref[:, h * tail : (h + 1) * tail] = weights
        total = jnp.dot(weights, ones, preferred_element_type=jnp.float32)
        stat_ref[:, h : h + 1] = top
        stat_ref[:, COLS + h : COLS + h + 1] = total[:, 0:1]


def merge_kernel(
    counts, w_ref, mv_ref, acc_ref, own_ref, mot_ref, o_ref
):
    own_live = counts[0] * FT
    tail = mv_ref.shape[0]
    rows = pl.program_id(0) * TQ + lax.broadcasted_iota(jnp.int32, (TQ, 1), 0)
    row_live = rows < own_live
    for h in range(o_ref.shape[1] // HD):
        c = head_cols(h)
        acc_mot = jnp.dot(
            w_ref[:, h * tail : (h + 1) * tail],
            mv_ref[:, c],
            preferred_element_type=jnp.float32,
        )
        top_own = own_ref[:, h : h + 1]
        top_mot = mot_ref[:, h : h + 1]
        peak = jnp.maximum(top_own, top_mot)
        factor_own = jnp.exp(top_own - peak)
        factor_mot = jnp.exp(top_mot - peak)
        scale = 1.0 / (
            own_ref[:, COLS + h : COLS + h + 1] * factor_own
            + mot_ref[:, COLS + h : COLS + h + 1] * factor_mot
        )
        mixed = (acc_ref[:, c] * factor_own + acc_mot * factor_mot) * scale
        o_ref[:, c] = jnp.where(row_live, mixed, 0.0).astype(o_ref.dtype)


def rows_of(width):
    return pl.BlockSpec((TQ, width), lambda i, c: (i, 0))


def whole(rows, width):
    return pl.BlockSpec((rows, width), lambda i, c: (0, 0))


def call(kernel, counts, operands, in_specs, outs, cost):
    span = operands[0].shape[0]
    shapes = [jax.ShapeDtypeStruct((span, w), t) for w, t in outs]
    return pl.pallas_call(
        kernel,
        out_shape=tuple(shapes),
        grid_spec=pltpu.PrefetchScalarGridSpec(
            num_scalar_prefetch=1,
            grid=(span // TQ,),
            in_specs=in_specs,
            out_specs=[rows_of(w) for w, _ in outs],
        ),
        compiler_params=pltpu.CompilerParams(dimension_semantics=("arbitrary",)),
        cost_estimate=cost,
    )(counts, *operands)


def relay_plan(mesh):
    where = [mesh.devices[c, 0, 0].coords for c in range(mesh.devices.shape[0])]
    inner, first, second = [], [], []
    for c in range(1, len(where)):
        (xs, ys, zs), (xr, yr, zr) = where[c - 1], where[c]
        via = [j for j, (x, y, z) in enumerate(where) if y == ys and z == zr]
        if ys == yr or not via:
            inner.append((c - 1, c))
        else:
            first.append((c - 1, via[0]))
            second.append((via[0], c))
    return inner, first, second


def body(plan, queries, keys, values, frames, motion):
    stretch_index = lax.axis_index("stretch")
    tail = MOT_CAP * FT
    count_own = frames[stretch_index]
    counts = jnp.stack([count_own, motion[stretch_index]]).astype(jnp.int32)
    tail_begin = (count_own - MOT_CAP) * FT
    groups = lax.axis_size("head")
    rows, width = keys.shape
    local = width // groups

    def by_target(x):
        return x.reshape(rows, groups, local).transpose(1, 0, 2)

    kv_send = jnp.stack([by_target(keys), by_target(values)], axis=1)
    kv_recv = lax.all_to_all(kv_send, "head", split_axis=0, concat_axis=0, tiled=True)
    kv_rows = kv_recv.transpose(1, 0, 2, 3).reshape(2, groups * rows, local)
    k_heads, v_heads = kv_rows[0], kv_rows[1]
    k_tail = lax.dynamic_slice_in_dim(k_heads, tail_begin, tail, 0)
    v_tail = lax.dynamic_slice_in_dim(v_heads, tail_begin, tail, 0)
    k_prior = from_behind(k_tail, "stretch", 1)
    inner, first, second = plan
    half = tail // 4
    v_near = from_behind(v_tail[:half], "stretch", 1)
    v_far = v_tail[half:]
    if first:
        v_far = lax.ppermute(v_far, "stretch", inner) + lax.ppermute(
            lax.ppermute(v_far, "stretch", first), "stretch", second
        )
    else:
        v_far = from_behind(v_far, "stretch", 1)
    v_prior = jnp.concatenate([v_near, v_far], axis=0)
    q_heads = lax.all_to_all(queries, "head", split_axis=1, concat_axis=0, tiled=True)
    span, local = q_heads.shape
    heads = local // HD
    f32 = jnp.float32
    acc, own_stat = call(
        own_kernel,
        counts,
        (q_heads, k_heads, v_heads),
        [rows_of(local), whole(span, local), whole(span, local)],
        [(local, f32), (PAIR, f32)],
        pl.CostEstimate(
            flops=heads * 2 * span * span * 3 * HD,
            transcendentals=heads * span * span,
            bytes_accessed=3 * span * local * 2 + span * local * 4,
        ),
    )
    w_mot, mot_stat = call(
        mscore_kernel,
        counts,
        (q_heads, k_prior),
        [rows_of(local), whole(tail, local)],
        [(heads * tail, jnp.bfloat16), (PAIR, f32)],
        pl.CostEstimate(
            flops=heads * 2 * span * tail * 2 * HD,
            transcendentals=heads * span * tail,
            bytes_accessed=span * local * 2 + tail * local * 2 + span * heads * tail * 2,
        ),
    )
    (mixed,) = call(
        merge_kernel,
        counts,
        (w_mot, v_prior, acc, own_stat, mot_stat),
        [
            rows_of(heads * tail),
            whole(tail, local),
            rows_of(local),
            rows_of(PAIR),
            rows_of(PAIR),
        ],
        [(local, jnp.bfloat16)],
        pl.CostEstimate(
            flops=heads * 2 * span * tail * HD,
            transcendentals=2 * heads * span,
            bytes_accessed=span * heads * tail * 2 + span * local * 6 + tail * local * 2,
        ),
    )
    return lax.all_to_all(mixed, "head", split_axis=0, concat_axis=1, tiled=True)


def solution(mesh):
    placed = (
        P(("cfg", "stretch", "head"), None),
        P(("cfg", "stretch", "head"), None),
        P(("cfg", "stretch", "head"), None),
        P(),
        P(),
    )
    return jax.shard_map(
        functools.partial(body, relay_plan(mesh)),
        mesh=mesh,
        in_specs=placed,
        out_specs=P(("cfg", "stretch", "head"), None),
        check_vma=False,
    )
```

```python
import functools
import math

import jax
import jax.numpy as jnp
from jax import lax
from jax.experimental import pallas as pl
from jax.experimental.pallas import tpu as pltpu
from jax.sharding import PartitionSpec as P

HD = 128
FT = 128
MOT_CAP = 4

NEG = -1e30
TQ = 448
COLS = 8


def from_behind(shard, axis, by):
    size = lax.axis_size(axis)
    pairs = [(i, i + by) for i in range(size) if 0 <= i + by < size]
    return lax.ppermute(shard, axis, pairs)


def scaled_scores(q, k, live):
    scores = lax.dot_general(
        q, k, (((1,), (1,)), ((), ())), preferred_element_type=jnp.float32
    )
    scores = scores * (1.0 / math.sqrt(HD))
    return jnp.where(live, scores, NEG)


def head_cols(h):
    return slice(h * HD, (h + 1) * HD)


def own_kernel(counts, q_ref, k_ref, v_ref, acc_ref, top_ref, tot_ref):
    own_live = counts[0] * FT
    span = k_ref.shape[0]
    key_live = lax.broadcasted_iota(jnp.int32, (1, span), 1) < own_live
    for h in range(acc_ref.shape[1] // HD):
        c = head_cols(h)
        masked = scaled_scores(q_ref[:, c], k_ref[:, c], key_live)
        top = jnp.max(masked, axis=1, keepdims=True)
        weights = jnp.exp(masked - top).astype(jnp.bfloat16)
        v = v_ref[:, c]
        v_ext = jnp.concatenate([v, jnp.ones_like(v)], axis=1)
        both = jnp.dot(weights, v_ext, preferred_element_type=jnp.float32)
        acc_ref[:, c] = both[:, :HD].astype(acc_ref.dtype)
        top_ref[:, h : h + 1] = top
        tot_ref[:, h : h + 1] = both[:, HD : HD + 1]


def mscore_kernel(counts, q_ref, mk_ref, w_ref, top_ref, tot_ref):
    mot_start = (MOT_CAP - counts[1]) * FT
    tail = mk_ref.shape[0]
    slot_live = lax.broadcasted_iota(jnp.int32, (1, tail), 1) >= mot_start
    ones = jnp.ones((tail, HD), jnp.bfloat16)
    for h in range(q_ref.shape[1] // HD):
        c = head_cols(h)
        masked = scaled_scores(q_ref[:, c], mk_ref[:, c], slot_live)
        top = jnp.max(masked, axis=1, keepdims=True)
        weights = jnp.exp(masked - top).astype(jnp.bfloat16)
        w_ref[:, h * tail : (h + 1) * tail] = weights
        total = jnp.dot(weights, ones, preferred_element_type=jnp.float32)
        top_ref[:, h : h + 1] = top
        tot_ref[:, h : h + 1] = total[:, 0:1]


def merge_kernel(
    counts, w_ref, mv_ref, acc_ref, top_ref, tot_ref, mtop_ref, mtot_ref, o_ref
):
    own_live = counts[0] * FT
    tail = mv_ref.shape[0]
    rows = pl.program_id(0) * TQ + lax.broadcasted_iota(jnp.int32, (TQ, 1), 0)
    row_live = rows < own_live
    for h in range(o_ref.shape[1] // HD):
        c = head_cols(h)
        acc_mot = jnp.dot(
            w_ref[:, h * tail : (h + 1) * tail],
            mv_ref[:, c],
            preferred_element_type=jnp.float32,
        )
        top_own = top_ref[:, h : h + 1]
        top_mot = mtop_ref[:, h : h + 1]
        peak = jnp.maximum(top_own, top_mot)
        factor_own = jnp.exp(top_own - peak)
        factor_mot = jnp.exp(top_mot - peak)
        scale = 1.0 / (
            tot_ref[:, h : h + 1] * factor_own + mtot_ref[:, h : h + 1] * factor_mot
        )
        mixed = (acc_ref[:, c].astype(jnp.float32) * factor_own + acc_mot * factor_mot) * scale
        o_ref[:, c] = jnp.where(row_live, mixed, 0.0).astype(o_ref.dtype)


def rows_of(width):
    return pl.BlockSpec((TQ, width), lambda i, c: (i, 0))


def whole(rows, width):
    return pl.BlockSpec((rows, width), lambda i, c: (0, 0))


def call(kernel, counts, operands, in_specs, outs, cost):
    span = operands[0].shape[0]
    shapes = [jax.ShapeDtypeStruct((span, w), t) for w, t in outs]
    return pl.pallas_call(
        kernel,
        out_shape=tuple(shapes),
        grid_spec=pltpu.PrefetchScalarGridSpec(
            num_scalar_prefetch=1,
            grid=(span // TQ,),
            in_specs=in_specs,
            out_specs=[rows_of(w) for w, _ in outs],
        ),
        compiler_params=pltpu.CompilerParams(dimension_semantics=("arbitrary",)),
        cost_estimate=cost,
    )(counts, *operands)


def relay_plan(mesh):
    where = [mesh.devices[c, 0, 0].coords for c in range(mesh.devices.shape[0])]
    inner, first, second = [], [], []
    for c in range(1, len(where)):
        (xs, ys, zs), (xr, yr, zr) = where[c - 1], where[c]
        via = [j for j, (x, y, z) in enumerate(where) if y == ys and z == zr]
        if ys == yr or not via:
            inner.append((c - 1, c))
        else:
            first.append((c - 1, via[0]))
            second.append((via[0], c))
    return inner, first, second


def body(plan, queries, keys, values, frames, motion):
    stretch_index = lax.axis_index("stretch")
    tail = MOT_CAP * FT
    count_own = frames[stretch_index]
    counts = jnp.stack([count_own, motion[stretch_index]]).astype(jnp.int32)
    tail_begin = (count_own - MOT_CAP) * FT
    groups = lax.axis_size("head")
    rows, width = keys.shape
    local = width // groups

    def by_target(x):
        return x.reshape(rows, groups, local).transpose(1, 0, 2)

    kv_send = jnp.stack([by_target(keys), by_target(values)], axis=1)
    kv_recv = lax.all_to_all(kv_send, "head", split_axis=0, concat_axis=0, tiled=True)
    kv_rows = kv_recv.transpose(1, 0, 2, 3).reshape(2, groups * rows, local)
    k_heads, v_heads = kv_rows[0], kv_rows[1]
    k_tail = lax.dynamic_slice_in_dim(k_heads, tail_begin, tail, 0)
    v_tail = lax.dynamic_slice_in_dim(v_heads, tail_begin, tail, 0)
    k_prior = from_behind(k_tail, "stretch", 1)
    inner, first, second = plan
    half = tail // 4
    v_near = from_behind(v_tail[:half], "stretch", 1)
    v_far = v_tail[half:]
    if first:
        v_far = lax.ppermute(v_far, "stretch", inner) + lax.ppermute(
            lax.ppermute(v_far, "stretch", first), "stretch", second
        )
    else:
        v_far = from_behind(v_far, "stretch", 1)
    v_prior = jnp.concatenate([v_near, v_far], axis=0)
    q_heads = lax.all_to_all(queries, "head", split_axis=1, concat_axis=0, tiled=True)
    span, local = q_heads.shape
    heads = local // HD
    f32 = jnp.float32
    acc, top, tot = call(
        own_kernel,
        counts,
        (q_heads, k_heads, v_heads),
        [rows_of(local), whole(span, local), whole(span, local)],
        [(local, jnp.bfloat16), (COLS, f32), (COLS, f32)],
        pl.CostEstimate(
            flops=heads * 2 * span * span * 3 * HD,
            transcendentals=heads * span * span,
            bytes_accessed=3 * span * local * 2 + span * local * 4,
        ),
    )
    w_mot, mtop, mtot = call(
        mscore_kernel,
        counts,
        (q_heads, k_prior),
        [rows_of(local), whole(tail, local)],
        [(heads * tail, jnp.bfloat16), (COLS, f32), (COLS, f32)],
        pl.CostEstimate(
            flops=heads * 2 * span * tail * 2 * HD,
            transcendentals=heads * span * tail,
            bytes_accessed=span * local * 2 + tail * local * 2 + span * heads * tail * 2,
        ),
    )
    (mixed,) = call(
        merge_kernel,
        counts,
        (w_mot, v_prior, acc, top, tot, mtop, mtot),
        [
            rows_of(heads * tail),
            whole(tail, local),
            rows_of(local),
            rows_of(COLS),
            rows_of(COLS),
            rows_of(COLS),
            rows_of(COLS),
        ],
        [(local, jnp.bfloat16)],
        pl.CostEstimate(
            flops=heads * 2 * span * tail * HD,
            transcendentals=2 * heads * span,
            bytes_accessed=span * heads * tail * 2 + span * local * 6 + tail * local * 2,
        ),
    )
    return lax.all_to_all(mixed, "head", split_axis=0, concat_axis=1, tiled=True)


def solution(mesh):
    placed = (
        P(("cfg", "stretch", "head"), None),
        P(("cfg", "stretch", "head"), None),
        P(("cfg", "stretch", "head"), None),
        P(),
        P(),
    )
    return jax.shard_map(
        functools.partial(body, relay_plan(mesh)),
        mesh=mesh,
        in_specs=placed,
        out_specs=P(("cfg", "stretch", "head"), None),
        check_vma=False,
    )
```

```python
import functools
import math

import jax
import jax.numpy as jnp
from jax import lax
from jax.experimental import pallas as pl
from jax.experimental.pallas import tpu as pltpu
from jax.sharding import PartitionSpec as P

HD = 128
FT = 128
MOT_CAP = 4

NEG = -1e30
TQ = 448
COLS = 8


def from_behind(shard, axis, by):
    size = lax.axis_size(axis)
    pairs = [(i, i + by) for i in range(size) if 0 <= i + by < size]
    return lax.ppermute(shard, axis, pairs)


def scaled_scores(q, k, live):
    scores = lax.dot_general(
        q, k, (((1,), (1,)), ((), ())), preferred_element_type=jnp.float32
    )
    scores = scores * (1.0 / math.sqrt(HD))
    return jnp.where(live, scores, NEG)


def head_cols(h):
    return slice(h * HD, (h + 1) * HD)


def own_kernel(counts, q_ref, k_ref, v_ref, acc_ref, top_ref, tot_ref):
    own_live = counts[0] * FT
    span = k_ref.shape[0]
    key_live = lax.broadcasted_iota(jnp.int32, (1, span), 1) < own_live
    for h in range(acc_ref.shape[1] // HD):
        c = head_cols(h)
        masked = scaled_scores(q_ref[:, c], k_ref[:, c], key_live)
        top = jnp.max(masked, axis=1, keepdims=True)
        weights = jnp.exp(masked - top).astype(jnp.bfloat16)
        v = v_ref[:, c]
        v_ext = jnp.concatenate([v, jnp.ones_like(v)], axis=1)
        both = jnp.dot(weights, v_ext, preferred_element_type=jnp.float32)
        acc_ref[:, c] = both[:, :HD]
        top_ref[:, h : h + 1] = top
        tot_ref[:, h : h + 1] = both[:, HD : HD + 1]


def mscore_kernel(counts, q_ref, mk_ref, w_ref, top_ref, tot_ref):
    mot_start = (MOT_CAP - counts[1]) * FT
    tail = mk_ref.shape[0]
    slot_live = lax.broadcasted_iota(jnp.int32, (1, tail), 1) >= mot_start
    ones = jnp.ones((tail, HD), jnp.bfloat16)
    for h in range(q_ref.shape[1] // HD):
        c = head_cols(h)
        masked = scaled_scores(q_ref[:, c], mk_ref[:, c], slot_live)
        top = jnp.max(masked, axis=1, keepdims=True)
        weights = jnp.exp(masked - top).astype(jnp.bfloat16)
        w_ref[:, h * tail : (h + 1) * tail] = weights
        total = jnp.dot(weights, ones, preferred_element_type=jnp.float32)
        top_ref[:, h : h + 1] = top
        tot_ref[:, h : h + 1] = total[:, 0:1]


def merge_kernel(
    counts, w_ref, mv_ref, acc_ref, top_ref, tot_ref, mtop_ref, mtot_ref, o_ref
):
    own_live = counts[0] * FT
    tail = mv_ref.shape[0]
    rows = pl.program_id(0) * TQ + lax.broadcasted_iota(jnp.int32, (TQ, 1), 0)
    row_live = rows < own_live
    for h in range(o_ref.shape[1] // HD):
        c = head_cols(h)
        acc_mot = jnp.dot(
            w_ref[:, h * tail : (h + 1) * tail],
            mv_ref[:, c],
            preferred_element_type=jnp.float32,
        )
        top_own = top_ref[:, h : h + 1]
        top_mot = mtop_ref[:, h : h + 1]
        peak = jnp.maximum(top_own, top_mot)
        factor_own = jnp.exp(top_own - peak)
        factor_mot = jnp.exp(top_mot - peak)
        scale = 1.0 / (
            tot_ref[:, h : h + 1] * factor_own + mtot_ref[:, h : h + 1] * factor_mot
        )
        mixed = (acc_ref[:, c] * factor_own + acc_mot * factor_mot) * scale
        o_ref[:, c] = jnp.where(row_live, mixed, 0.0).astype(o_ref.dtype)


def rows_of(width):
    return pl.BlockSpec((TQ, width), lambda i, c: (i, 0))


def whole(rows, width):
    return pl.BlockSpec((rows, width), lambda i, c: (0, 0))


def call(kernel, counts, operands, in_specs, outs, cost):
    span = operands[0].shape[0]
    shapes = [jax.ShapeDtypeStruct((span, w), t) for w, t in outs]
    return pl.pallas_call(
        kernel,
        out_shape=tuple(shapes),
        grid_spec=pltpu.PrefetchScalarGridSpec(
            num_scalar_prefetch=1,
            grid=(span // TQ,),
            in_specs=in_specs,
            out_specs=[rows_of(w) for w, _ in outs],
        ),
        compiler_params=pltpu.CompilerParams(dimension_semantics=("arbitrary",)),
        cost_estimate=cost,
    )(counts, *operands)


def relay_plan(mesh):
    where = [mesh.devices[c, 0, 0].coords for c in range(mesh.devices.shape[0])]
    inner, first, second = [], [], []
    for c in range(1, len(where)):
        (xs, ys, zs), (xr, yr, zr) = where[c - 1], where[c]
        via = [j for j, (x, y, z) in enumerate(where) if y == ys and z == zr]
        if ys == yr or not via:
            inner.append((c - 1, c))
        else:
            first.append((c - 1, via[0]))
            second.append((via[0], c))
    return inner, first, second


def body(plan, queries, keys, values, frames, motion):
    stretch_index = lax.axis_index("stretch")
    tail = MOT_CAP * FT
    count_own = frames[stretch_index]
    counts = jnp.stack([count_own, motion[stretch_index]]).astype(jnp.int32)
    tail_begin = (count_own - MOT_CAP) * FT
    groups = lax.axis_size("head")
    rows, width = keys.shape
    local = width // groups

    def by_target(x):
        return x.reshape(rows, groups, local).transpose(1, 0, 2)

    kv_send = jnp.stack([by_target(keys), by_target(values)], axis=1)
    kv_recv = lax.all_to_all(kv_send, "head", split_axis=0, concat_axis=0, tiled=True)
    kv_rows = kv_recv.transpose(1, 0, 2, 3).reshape(2, groups * rows, local)
    k_heads, v_heads = kv_rows[0], kv_rows[1]
    k_tail = lax.dynamic_slice_in_dim(k_heads, tail_begin, tail, 0)
    v_tail = lax.dynamic_slice_in_dim(v_heads, tail_begin, tail, 0)
    k_prior = from_behind(k_tail, "stretch", 1)
    inner, first, second = plan
    half = 5 * tail // 16
    v_near = from_behind(v_tail[:half], "stretch", 1)
    v_far = v_tail[half:]
    if first:
        v_far = lax.ppermute(v_far, "stretch", inner) + lax.ppermute(
            lax.ppermute(v_far, "stretch", first), "stretch", second
        )
    else:
        v_far = from_behind(v_far, "stretch", 1)
    v_prior = jnp.concatenate([v_near, v_far], axis=0)
    q_heads = lax.all_to_all(queries, "head", split_axis=1, concat_axis=0, tiled=True)
    span, local = q_heads.shape
    heads = local // HD
    f32 = jnp.float32
    acc, top, tot = call(
        own_kernel,
        counts,
        (q_heads, k_heads, v_heads),
        [rows_of(local), whole(span, local), whole(span, local)],
        [(local, f32), (COLS, f32), (COLS, f32)],
        pl.CostEstimate(
            flops=heads * 2 * span * span * 3 * HD,
            transcendentals=heads * span * span,
            bytes_accessed=3 * span * local * 2 + span * local * 4,
        ),
    )
    w_mot, mtop, mtot = call(
        mscore_kernel,
        counts,
        (q_heads, k_prior),
        [rows_of(local), whole(tail, local)],
        [(heads * tail, jnp.bfloat16), (COLS, f32), (COLS, f32)],
        pl.CostEstimate(
            flops=heads * 2 * span * tail * 2 * HD,
            transcendentals=heads * span * tail,
            bytes_accessed=span * local * 2 + tail * local * 2 + span * heads * tail * 2,
        ),
    )
    (mixed,) = call(
        merge_kernel,
        counts,
        (w_mot, v_prior, acc, top, tot, mtop, mtot),
        [
            rows_of(heads * tail),
            whole(tail, local),
            rows_of(local),
            rows_of(COLS),
            rows_of(COLS),
            rows_of(COLS),
            rows_of(COLS),
        ],
        [(local, jnp.bfloat16)],
        pl.CostEstimate(
            flops=heads * 2 * span * tail * HD,
            transcendentals=2 * heads * span,
            bytes_accessed=span * heads * tail * 2 + span * local * 6 + tail * local * 2,
        ),
    )
    return lax.all_to_all(mixed, "head", split_axis=0, concat_axis=1, tiled=True)


def solution(mesh):
    placed = (
        P(("cfg", "stretch", "head"), None),
        P(("cfg", "stretch", "head"), None),
        P(("cfg", "stretch", "head"), None),
        P(),
        P(),
    )
    return jax.shard_map(
        functools.partial(body, relay_plan(mesh)),
        mesh=mesh,
        in_specs=placed,
        out_specs=P(("cfg", "stretch", "head"), None),
        check_vma=False,
    )
```
